256 devices in a mesh: tm: 8 (over y, core), tile: 32 (over x, z).
Axes of the slice: x: 4, y: 4, z: 8, core: 2. Of those that a mesh axis runs over, the one named last changes fastest.
Arguments:
- transformer_output_units: bfloat16 [8, 5120, 128], P('tm', 'tile'), may hold values from -10 to 10
- packed_unit_lookup: int32 [8, 5120], P('tm', 'tile'), may hold values from 0 to 5119, as said below
- channel_latent_mean: float32 [16], replicated, may hold values from -3 to 3
- channel_latent_deviation: float32 [16], replicated, may hold values from 0.5 to 2
- entry_conv_weight: bfloat16 [3, 3, 3, 16, 384], replicated, may hold values from -0.6 to 0.6
- entry_conv_bias: float32 [384], replicated, may hold values from -3 to 3
- group_norm_gain: float32 [384], replicated, may hold values from 0.25 to 1.75
- group_norm_offset: float32 [384], replicated, may hold values from -3 to 3
- residual_conv_weight: bfloat16 [3, 3, 3, 384, 384], replicated, may hold values from -0.0625 to 0.0625
- residual_conv_bias: float32 [384], replicated, may hold values from -3 to 3
- enlarge_conv_weight: bfloat16 [3, 3, 192, 384], replicated, may hold values from -0.109375 to 0.109375
- enlarge_conv_bias: float32 [192], replicated, may hold values from -3 to 3
Outputs:
- frames_out: bfloat16 [16, 256, 160, 384], P('tm', 'tile')
The draws below stay inside these ranges and needn't reach their ends.
Inputs may be any that keep to these rules, and one draw needn't show every extreme that they name: `packed_unit_lookup`: each row (one time block) holds every number 0 to 5119 once; the unit at a column goes to tile v // 160, slot v % 160, v being the entry. Of the 160 columns of one device, at most 12 go to one tile; in every row some device sends exactly 12 to some tile, and all devices of a row send the same collection of per-tile counts, each in its own order.
All inputs are finite; a program needn't handle non-finite values.
Results may differ from the reference program's by a relative error of at most 0.006.
The reference program's roundings to bfloat16 on the way (of `raw_latent`, `latent`, `hidden`, `activated`, `residual` and `phase_weight`) count: a program that leaves them out, or rounds other values in their place, can miss the bound.
Values may be sent and summed in bfloat16 or wider, within the bound.
No kernel may reach another device: no remote copies, remote signals or barrier semaphores. Data moves between devices by JAX's collectives and lax.ppermute only.
A program may use at most 64 MiB of HBM per device.

```python
import math
from functools import partial
import jax
import jax.numpy as jnp
from jax import lax

C = 384
ZC = 16
G = 32
W = 160
FR_DEV = 2
TH = 4
CO = 192
BLOCKS = 8
TILES = 32
FRAMES = 16
ROWS = 128
UNITS = 160
CAP = 12
PAIR = 128


def color_counts(seed_key):
    first_color = jax.random.randint(jax.random.fold_in(seed_key, 1), (), 0, TILES)
    colors = jnp.arange(TILES, dtype=jnp.int32)
    counts = jnp.where(colors == first_color, CAP, 0).astype(jnp.int32)

    def place_one(turn_index, current):
        scores = jax.random.randint(jax.random.fold_in(seed_key, 100 + turn_index), (TILES,), 0, 1 << 20) * TILES + colors
        usable = (current < CAP) & (colors != first_color)
        chosen = jnp.argmax(jnp.where(usable, scores, -1))
        return current + (colors == chosen).astype(jnp.int32)
    return lax.fori_loop(0, UNITS - CAP, place_one, counts)


def unit_order(row_key):
    return jax.random.permutation(row_key, UNITS).astype(jnp.int32)


def block_targets(seed_key):
    counts = color_counts(seed_key)
    row_shift = jax.random.permutation(jax.random.fold_in(seed_key, 2), TILES)
    col_shift = jax.random.permutation(jax.random.fold_in(seed_key, 3), TILES)
    pair_count = counts[(row_shift[:, None] + col_shift[None, :]) % TILES]
    row_end = jnp.cumsum(pair_count, axis=1)
    row_start = row_end - pair_count
    col_start = jnp.cumsum(pair_count, axis=0) - pair_count
    unit_ranks = jnp.arange(UNITS, dtype=jnp.int32)
    target_tile = jnp.sum((row_end[:, None, :] <= unit_ranks[None, :, None]).astype(jnp.int32), axis=2)
    offset_in = unit_ranks[None, :] - jnp.take_along_axis(row_start, target_tile, axis=1)
    slot_orders = jax.vmap(unit_order)(jax.random.split(jax.random.fold_in(seed_key, 4), TILES))
    slot_pick = jnp.take_along_axis(col_start, target_tile, axis=1) + offset_in
    target_slot = slot_orders[target_tile, slot_pick]
    position_orders = jax.vmap(unit_order)(jax.random.split(jax.random.fold_in(seed_key, 5), TILES))
    sources = jnp.broadcast_to(jnp.arange(TILES, dtype=jnp.int32)[:, None], (TILES, UNITS))
    positioned_units = jnp.zeros((TILES, UNITS), jnp.int32).at[sources, position_orders].set(target_tile * UNITS + target_slot)
    return positioned_units.reshape(TILES * UNITS)


def block_table(seed_key):
    block_keys = jax.vmap(partial(jax.random.fold_in, seed_key))(jnp.arange(BLOCKS, dtype=jnp.int32))
    return jax.vmap(block_targets)(block_keys)


def draw_packed_unit_lookup(key, part):
    return block_table(jax.random.fold_in(key, 77))


def draw_transformer_output_units(key, part):
    targets = block_table(jax.random.fold_in(key, 77))
    target_tile = targets // UNITS
    target_slot = targets % UNITS
    frame_local = target_slot // (TH // 2 * (W // 4))
    unit_row = target_slot // (W // 4) % (TH // 2)
    unit_col = target_slot % (W // 4)
    frame_global = jnp.arange(BLOCKS, dtype=jnp.int32)[:, None] * FR_DEV + frame_local
    value_index = jnp.arange(PAIR, dtype=jnp.int32)
    row_global = (target_tile * TH + 2 * unit_row)[:, :, None] + value_index // (2 * ZC) % 2
    col_global = (4 * unit_col)[:, :, None] + 2 * (value_index // (4 * ZC)) + value_index // ZC % 2
    time_part = (frame_global.astype(jnp.float32) / (FRAMES - 1))[:, :, None]
    tile_amp = jnp.exp(jax.random.uniform(jax.random.fold_in(key, 11), (BLOCKS, TILES), jnp.float32, 0.0, math.log(4.0)))
    tile_part = jnp.take_along_axis(tile_amp, target_tile, axis=1)[:, :, None]
    row_rough = jnp.exp(jax.random.uniform(jax.random.fold_in(key, 12), (ROWS,), jnp.float32, math.log(0.6), math.log(1.6)))
    col_rough = jnp.exp(jax.random.uniform(jax.random.fold_in(key, 13), (W,), jnp.float32, math.log(0.6), math.log(1.6)))
    scales = 0.065 * 4.0 ** time_part * tile_part * jnp.take(row_rough, row_global) * jnp.take(col_rough, col_global)
    shape_all = (BLOCKS, TILES * UNITS, PAIR)
    noise_key = jax.random.fold_in(key, 5)
    values = jax.random.truncated_normal(noise_key, -3.5, 3.5, shape_all, jnp.float32)
    return (values * scales).astype(jnp.bfloat16)


def draw_entry_conv_weight(key, part):
    base_draw = jax.random.truncated_normal(jax.random.fold_in(key, 1), -4.0, 4.0, (3, 3, 3, ZC, C), jnp.float32) * (27 * ZC) ** (-0.5)
    channel_scale = jnp.exp(jax.random.uniform(jax.random.fold_in(key, 2), (C,), jnp.float32, math.log(0.3), math.log(3.0)))
    return (base_draw * channel_scale).astype(jnp.bfloat16)


def gaussian(key, extent, spread, most, kind=jnp.bfloat16):
    result = jax.random.normal(key, extent, jnp.float32) * spread
    return jnp.minimum(jnp.maximum(result, -most), most).astype(kind)


def setup_inputs(seed: int = 0) -> dict:
    arg_keys = jax.random.split(jax.random.key(seed), 13)
    return {
        "transformer_output_units": draw_transformer_output_units(jax.random.fold_in(arg_keys[12], 71), 0),
        "packed_unit_lookup": draw_packed_unit_lookup(jax.random.fold_in(arg_keys[12], 71), 0),
        "channel_latent_mean": gaussian(arg_keys[2], (ZC,), 0.5, 3.0, jnp.float32),
        "channel_latent_deviation": jnp.clip(jnp.exp(jax.random.uniform(arg_keys[3], (ZC,), jnp.float32, math.log(0.5), math.log(2.0))), 0.5, 2.0),
        "entry_conv_weight": draw_entry_conv_weight(jax.random.fold_in(arg_keys[12], 71), 0),
        "entry_conv_bias": gaussian(arg_keys[5], (C,), 0.3, 3.0, jnp.float32),
        "group_norm_gain": jnp.clip(1.0 + 0.15 * jax.random.normal(arg_keys[6], (C,), jnp.float32), 0.25, 1.75),
        "group_norm_offset": gaussian(arg_keys[7], (C,), 0.5, 3.0, jnp.float32),
        "residual_conv_weight": gaussian(arg_keys[8], (3, 3, 3, C, C), (27 * C) ** -0.5, 0.0625),
        "residual_conv_bias": gaussian(arg_keys[9], (C,), 0.3, 3.0, jnp.float32),
        "enlarge_conv_weight": gaussian(arg_keys[10], (3, 3, CO, C), (9 * C) ** -0.5, 0.109375),
        "enlarge_conv_bias": gaussian(arg_keys[11], (CO,), 0.3, 3.0, jnp.float32),
    }


def causal_conv(features, weight, add_bias):
    frame_count, row_count, col_count, channel_in = features.shape
    padded = jnp.pad(features, ((2, 0), (1, 1), (1, 1), (0, 0)))

    def one_frame(frame_index):
        window = lax.dynamic_slice_in_dim(padded, frame_index, 3, 0)
        running = jnp.zeros((row_count * col_count, weight.shape[-1]), jnp.float32)
        for time_tap in range(3):
            for row_tap in range(3):
                for col_tap in range(3):
                    patch_rows = window[time_tap, row_tap:row_tap + row_count, col_tap:col_tap + col_count].reshape(row_count * col_count, channel_in)
                    running = running + jnp.dot(patch_rows, weight[time_tap, row_tap, col_tap], preferred_element_type=jnp.float32)
        return (running + add_bias).reshape(row_count, col_count, -1)
    return lax.map(one_frame, jnp.arange(frame_count, dtype=jnp.int32))

def phase_weights(enlarge_conv_weight):
    wide = enlarge_conv_weight.astype(jnp.float32)
    tap_groups = (((0,), (1, 2)), ((0, 1), (2,)))
    rows_a = []
    for row_phase in range(2):
        rows_b = []
        for col_phase in range(2):
            rows_u = []
            for row_off in range(2):
                rows_v = []
                for col_off in range(2):
                    total = jnp.zeros(wide.shape[2:], jnp.float32)
                    for row_tap in tap_groups[row_phase][row_off]:
                        for col_tap in tap_groups[col_phase][col_off]:
                            total = total + wide[row_tap, col_tap]
                    rows_v.append(total)
                rows_u.append(jnp.stack(rows_v))
            rows_b.append(jnp.stack(rows_u))
        rows_a.append(jnp.stack(rows_b))
    return jnp.stack(rows_a).astype(jnp.bfloat16)

def upsample_conv(features, enlarge_conv_weight, enlarge_conv_bias):
    frame_count, row_count, col_count, channels = features.shape
    phase_weight = phase_weights(enlarge_conv_weight)

    def one_image(image_rows):
        padded = jnp.pad(image_rows, ((1, 1), (1, 1), (0, 0)))
        row_phases = []
        for row_phase in range(2):
            halves = []
            for col_phase in range(2):
                running = jnp.zeros((row_count * col_count, phase_weight.shape[4]), jnp.float32)
                for row_off in range(2):
                    for col_off in range(2):
                        top = row_phase + row_off
                        left = col_phase + col_off
                        patch_rows = padded[top:top + row_count, left:left + col_count].reshape(-1, channels)
                        running = running + jnp.dot(patch_rows, phase_weight[row_phase, col_phase, row_off, col_off].T, preferred_element_type=jnp.float32)
                halves.append((running + enlarge_conv_bias).reshape(row_count, col_count, -1))
            row_phases.append(jnp.concatenate(halves, axis=2).astype(jnp.bfloat16))
        return jnp.stack(row_phases, axis=1).reshape(2 * row_count, col_count, -1)
    return lax.map(one_image, features)

def reference(transformer_output_units, packed_unit_lookup, channel_latent_mean, channel_latent_deviation, entry_conv_weight, entry_conv_bias, group_norm_gain, group_norm_offset, residual_conv_weight, residual_conv_bias, enlarge_conv_weight, enlarge_conv_bias):
    time_block_total = transformer_output_units.shape[0]
    positioned_units = jnp.zeros_like(transformer_output_units).at[jnp.arange(time_block_total, dtype=jnp.int32)[:, None], packed_unit_lookup].set(transformer_output_units)
    unit_grid = positioned_units.reshape(time_block_total, TILES, FR_DEV, TH // 2, W // 4, 2, 2, 2, ZC)
    raw_latent = unit_grid.transpose(0, 2, 1, 3, 6, 4, 5, 7, 8).reshape(FRAMES, ROWS, W, ZC)
    latent = (raw_latent.astype(jnp.float32) * channel_latent_deviation + channel_latent_mean).astype(jnp.bfloat16)
    hidden = causal_conv(latent, entry_conv_weight, entry_conv_bias).astype(jnp.bfloat16)
    grouped = hidden.astype(jnp.float32).reshape(FRAMES, ROWS * W, G, C // G)
    run_sum = jnp.cumsum(lax.optimization_barrier(jnp.sum(grouped, axis=(1, 3))), axis=0)
    run_square = jnp.cumsum(lax.optimization_barrier(jnp.sum(grouped * grouped, axis=(1, 3))), axis=0)
    cell_count = ((jnp.arange(FRAMES, dtype=jnp.int32) + 1) * (ROWS * W * (C // G))).astype(jnp.float32)[:, None]
    group_mean = run_sum / cell_count
    group_var = run_square / cell_count - group_mean * group_mean
    group_scale = lax.rsqrt(group_var + 1e-05)
    mean_wide = jnp.repeat(group_mean, C // G, axis=1)[:, None, None, :]
    scale_wide = jnp.repeat(group_scale, C // G, axis=1)[:, None, None, :]
    scaled = (hidden.astype(jnp.float32) - mean_wide) * scale_wide * group_norm_gain + group_norm_offset
    activated = jax.nn.silu(scaled).astype(jnp.bfloat16)
    residual = (hidden.astype(jnp.float32) + causal_conv(activated, residual_conv_weight, residual_conv_bias)).astype(jnp.bfloat16)
    return upsample_conv(residual, enlarge_conv_weight, enlarge_conv_bias)
```

```python
import jax
import jax.numpy as jnp
from jax import lax
from jax.sharding import PartitionSpec as P

C = 384
ZC = 16
G = 32
W = 160
FR_DEV = 2
TH = 4


def spatial_columns(framed, row_count, col_count, row_moves, col_moves):
    widened = jnp.pad(framed, ((0, 0), (0, 0), (1, 1), (0, 0)))
    return jnp.concatenate(
        [
            widened[
                :, 1 + row_move : 1 + row_move + row_count, 1 + col_move : 1 + col_move + col_count
            ]
            for row_move in row_moves
            for col_move in col_moves
        ],
        axis=3,
    )


def causal_conv(framed, weight, add_bias):
    frame_count = framed.shape[0] - 2
    row_count = framed.shape[1] - 2
    col_count = framed.shape[2]
    columns = spatial_columns(framed, row_count, col_count, (-1, 0, 1), (-1, 0, 1))
    flat_weight = weight.reshape(3, -1, weight.shape[-1])
    running = None
    for time_tap in range(3):
        tap_term = jnp.dot(
            columns[time_tap : time_tap + frame_count],
            flat_weight[time_tap],
            preferred_element_type=jnp.float32,
        )
        running = tap_term if running is None else running + tap_term
    return running + add_bias


def phase_weights(enlarge_conv_weight):
    wide = enlarge_conv_weight.astype(jnp.float32)
    tap_groups = (((0,), (1, 2)), ((0, 1), (2,)))
    rows_a = []
    for row_phase in range(2):
        rows_b = []
        for col_phase in range(2):
            rows_u = []
            for row_off in range(2):
                rows_v = []
                for col_off in range(2):
                    total = jnp.zeros(wide.shape[2:], jnp.float32)
                    for row_tap in tap_groups[row_phase][row_off]:
                        for col_tap in tap_groups[col_phase][col_off]:
                            total = total + wide[row_tap, col_tap]
                    rows_v.append(total)
                rows_u.append(jnp.stack(rows_v))
            rows_b.append(jnp.stack(rows_u))
        rows_a.append(jnp.stack(rows_b))
    return jnp.stack(rows_a).astype(jnp.bfloat16)


def upsample_conv(framed, enlarge_conv_weight, enlarge_conv_bias):
    frame_count = framed.shape[0]
    row_count = framed.shape[1] - 2
    col_count = framed.shape[2]
    channels = framed.shape[3]
    out_channels = enlarge_conv_weight.shape[2]
    phase_weight = phase_weights(enlarge_conv_weight)
    row_phases = []
    for row_phase in range(2):
        halves = []
        for col_phase in range(2):
            row_moves = [row_phase - 1 + row_off for row_off in range(2)]
            col_moves = [col_phase - 1 + col_off for col_off in range(2)]
            columns = spatial_columns(framed, row_count, col_count, row_moves, col_moves)
            flat_weight = (
                phase_weight[row_phase, col_phase]
                .transpose(0, 1, 3, 2)
                .reshape(4 * channels, out_channels)
            )
            halves.append(
                jnp.dot(columns, flat_weight, preferred_element_type=jnp.float32)
                + enlarge_conv_bias
            )
        row_phases.append(jnp.concatenate(halves, axis=3).astype(jnp.bfloat16))
    return jnp.stack(row_phases, axis=2).reshape(
        frame_count, 2 * row_count, col_count, 2 * out_channels
    )


def halo_latent(latent, reach):
    tm_count = lax.axis_size("tm")
    tile_count = lax.axis_size("tile")
    rows = latent.shape[1]
    pieces = {
        -1: lax.slice_in_dim(latent, 0, reach, axis=1),
        0: latent,
        1: lax.slice_in_dim(latent, rows - reach, rows, axis=1),
    }
    frame_blocks = []
    for back in (2, 1, 0):
        row_parts = []
        for side in (1, 0, -1):
            if back == 0 and side == 0:
                row_parts.append(latent)
                continue
            pairs = []
            for k in range(tm_count - back):
                for j in range(tile_count):
                    if 0 <= j + side < tile_count:
                        pairs.append((k * tile_count + j, (k + back) * tile_count + j + side))
            row_parts.append(lax.ppermute(pieces[side], ("tm", "tile"), pairs))
        frame_blocks.append(jnp.concatenate(row_parts, axis=1))
    return jnp.concatenate(frame_blocks, axis=0)


def frame_statistics(own_hidden, row_total):
    frame_count = own_hidden.shape[0]
    block_total = lax.axis_size("tm")
    block_index = lax.axis_index("tm")
    grouped = own_hidden.astype(jnp.float32).reshape(frame_count, -1, G, C // G)
    local = jnp.stack(
        [jnp.sum(grouped, axis=(1, 3)), jnp.sum(grouped * grouped, axis=(1, 3))]
    )
    frame_total = frame_count * block_total
    placed = lax.dynamic_update_slice(
        jnp.zeros((2, frame_total, G), jnp.float32), local, (0, block_index * frame_count, 0)
    )
    totals = lax.psum(placed, ("tm", "tile"))
    running = jnp.concatenate(
        [jnp.zeros((2, 2, G), jnp.float32), jnp.cumsum(totals, axis=1)], axis=1
    )
    window = lax.dynamic_slice_in_dim(running, block_index * frame_count, frame_count + 2, axis=1)
    frame_index = block_index * frame_count - 2 + jnp.arange(frame_count + 2, dtype=jnp.int32)
    cell_count = (
        jnp.maximum(frame_index + 1, 1) * (row_total * own_hidden.shape[2] * (C // G))
    ).astype(jnp.float32)[:, None]
    group_mean = window[0] / cell_count
    group_var = window[1] / cell_count - group_mean * group_mean
    return (group_mean, lax.rsqrt(jnp.maximum(group_var, 0.0) + 1e-05))


def normalize(features, group_mean, group_scale, group_norm_gain, group_norm_offset):
    repeat_count = features.shape[3] // group_mean.shape[1]
    mean_wide = jnp.repeat(group_mean, repeat_count, axis=1)[:, None, None, :]
    scale_wide = jnp.repeat(group_scale, repeat_count, axis=1)[:, None, None, :]
    scaled = (
        features.astype(jnp.float32) - mean_wide
    ) * scale_wide * group_norm_gain + group_norm_offset
    return jax.nn.silu(scaled)


def inside_mask(frame_count, row_count, frame_start, row_start, row_total):
    frame_index = frame_start + jnp.arange(frame_count, dtype=jnp.int32)
    row_index = row_start + jnp.arange(row_count, dtype=jnp.int32)
    frame_ok = frame_index >= 0
    row_ok = (row_index >= 0) & (row_index < row_total)
    return (frame_ok[:, None] & row_ok[None, :])[:, :, None, None]


def per_device(
    transformer_output_units,
    packed_unit_lookup,
    channel_latent_mean,
    channel_latent_deviation,
    entry_conv_weight,
    entry_conv_bias,
    group_norm_gain,
    group_norm_offset,
    residual_conv_weight,
    residual_conv_bias,
    enlarge_conv_weight,
    enlarge_conv_bias,
):
    tile_total = lax.axis_size("tile")
    unit_count = packed_unit_lookup.shape[1]
    unit_width = transformer_output_units.shape[2]
    slot_cap = 5 * unit_count // (2 * tile_total)
    targets = packed_unit_lookup[0]
    target_tile = targets // unit_count
    target_slot = targets % unit_count
    tile_match = target_tile[:, None] == jnp.arange(tile_total, dtype=jnp.int32)[None, :]
    earlier_same = jnp.cumsum(tile_match.astype(jnp.int32), axis=0) - 1
    send_rank = jnp.sum(jnp.where(tile_match, earlier_same, 0), axis=1)
    send_index = target_tile * slot_cap + send_rank
    select_dispatch = (
        jnp.arange(tile_total * slot_cap, dtype=jnp.int32)[:, None] == send_index[None, :]
    )
    send_units = jnp.dot(
        select_dispatch.astype(jnp.bfloat16),
        transformer_output_units[0],
        preferred_element_type=jnp.float32,
    ).astype(jnp.bfloat16)
    send_slots = jnp.sum(jnp.where(select_dispatch, target_slot[None, :] + 1, 0), axis=1)
    slot_lane = jnp.pad(
        send_slots.reshape(tile_total, slot_cap).astype(jnp.bfloat16),
        ((0, 0), (0, unit_width - slot_cap)),
    )
    packet = jnp.concatenate(
        [send_units.reshape(tile_total, slot_cap * unit_width), slot_lane], axis=1
    )
    got = lax.all_to_all(packet, "tile", split_axis=0, concat_axis=0, tiled=True)
    got_units = got[:, : slot_cap * unit_width].reshape(tile_total * slot_cap, unit_width)
    got_slots = got[:, slot_cap * unit_width : slot_cap * unit_width + slot_cap].astype(jnp.int32)
    choose_place = jnp.arange(1, unit_count + 1, dtype=jnp.int32)[:, None] == got_slots.reshape(
        1, -1
    )
    positioned_units = jnp.dot(
        choose_place.astype(jnp.bfloat16),
        got_units,
        preferred_element_type=jnp.float32,
    ).astype(jnp.bfloat16)
    unit_grid = positioned_units.reshape(FR_DEV, TH // 2, W // 4, 2, 2, 2, ZC)
    raw_latent = unit_grid.transpose(0, 1, 4, 2, 3, 5, 6).reshape(FR_DEV, TH, W, ZC)
    latent = (
        raw_latent.astype(jnp.float32) * channel_latent_deviation + channel_latent_mean
    ).astype(jnp.bfloat16)
    row_total = TH * tile_total
    frame_start = lax.axis_index("tm") * FR_DEV
    row_start = lax.axis_index("tile") * TH
    wide_latent = halo_latent(latent, 3)
    hidden = causal_conv(wide_latent, entry_conv_weight, entry_conv_bias).astype(jnp.bfloat16)
    group_mean, group_scale = frame_statistics(hidden[2:, 2 : 2 + TH], row_total)
    activated = jnp.where(
        inside_mask(FR_DEV + 2, TH + 4, frame_start - 2, row_start - 2, row_total),
        normalize(hidden, group_mean, group_scale, group_norm_gain, group_norm_offset),
        0.0,
    ).astype(jnp.bfloat16)
    residual = jnp.where(
        inside_mask(FR_DEV, TH + 2, frame_start, row_start - 1, row_total),
        hidden[2:, 1 : 3 + TH].astype(jnp.float32)
        + causal_conv(activated, residual_conv_weight, residual_conv_bias),
        0.0,
    ).astype(jnp.bfloat16)
    return upsample_conv(residual, enlarge_conv_weight, enlarge_conv_bias)


def solution(mesh):
    placed = (
        P("tm", "tile", None),
        P("tm", "tile"),
        P(),
        P(),
        P(),
        P(),
        P(),
        P(),
        P(),
        P(),
        P(),
        P(),
    )
    return jax.shard_map(
        per_device,
        mesh=mesh,
        in_specs=placed,
        out_specs=P("tm", "tile", None, None),
        check_vma=False,
    )
```

```python
import jax
import jax.numpy as jnp
from jax import lax
from jax.sharding import PartitionSpec as P

C = 384
ZC = 16
G = 32
W = 160
FR_DEV = 2
TH = 4


def spatial_columns(framed, row_count, col_count, row_moves, col_moves):
    widened = jnp.pad(framed, ((0, 0), (0, 0), (1, 1), (0, 0)))
    return jnp.concatenate(
        [
            widened[
                :, 1 + row_move : 1 + row_move + row_count, 1 + col_move : 1 + col_move + col_count
            ]
            for row_move in row_moves
            for col_move in col_moves
        ],
        axis=3,
    )


def causal_conv(framed, weight, add_bias):
    frame_count = framed.shape[0] - 2
    row_count = framed.shape[1] - 2
    col_count = framed.shape[2]
    columns = spatial_columns(framed, row_count, col_count, (-1, 0, 1), (-1, 0, 1))
    flat_weight = weight.reshape(3, -1, weight.shape[-1])
    running = None
    for time_tap in range(3):
        tap_term = jnp.dot(
            columns[time_tap : time_tap + frame_count],
            flat_weight[time_tap],
            preferred_element_type=jnp.float32,
        )
        running = tap_term if running is None else running + tap_term
    return running + add_bias


def phase_weights(enlarge_conv_weight):
    wide = enlarge_conv_weight.astype(jnp.float32)
    tap_groups = (((0,), (1, 2)), ((0, 1), (2,)))
    rows_a = []
    for row_phase in range(2):
        rows_b = []
        for col_phase in range(2):
            rows_u = []
            for row_off in range(2):
                rows_v = []
                for col_off in range(2):
                    total = jnp.zeros(wide.shape[2:], jnp.float32)
                    for row_tap in tap_groups[row_phase][row_off]:
                        for col_tap in tap_groups[col_phase][col_off]:
                            total = total + wide[row_tap, col_tap]
                    rows_v.append(total)
                rows_u.append(jnp.stack(rows_v))
            rows_b.append(jnp.stack(rows_u))
        rows_a.append(jnp.stack(rows_b))
    return jnp.stack(rows_a).astype(jnp.bfloat16)


def upsample_conv(framed, enlarge_conv_weight, enlarge_conv_bias):
    frame_count = framed.shape[0]
    row_count = framed.shape[1] - 2
    col_count = framed.shape[2]
    channels = framed.shape[3]
    out_channels = enlarge_conv_weight.shape[2]
    phase_weight = phase_weights(enlarge_conv_weight)
    row_phases = []
    for row_phase in range(2):
        halves = []
        for col_phase in range(2):
            row_moves = [row_phase - 1 + row_off for row_off in range(2)]
            col_moves = [col_phase - 1 + col_off for col_off in range(2)]
            columns = spatial_columns(framed, row_count, col_count, row_moves, col_moves)
            flat_weight = (
                phase_weight[row_phase, col_phase]
                .transpose(0, 1, 3, 2)
                .reshape(4 * channels, out_channels)
            )
            halves.append(
                jnp.dot(columns, flat_weight, preferred_element_type=jnp.float32)
                + enlarge_conv_bias
            )
        row_phases.append(jnp.concatenate(halves, axis=3).astype(jnp.bfloat16))
    return jnp.stack(row_phases, axis=2).reshape(
        frame_count, 2 * row_count, col_count, 2 * out_channels
    )


def neighbour_rows(latent, reach):
    tile_count = lax.axis_size("tile")
    rows = latent.shape[1]
    from_above = lax.ppermute(
        lax.slice_in_dim(latent, rows - reach, rows, axis=1),
        "tile",
        [(j, j + 1) for j in range(tile_count - 1)],
    )
    from_below = lax.ppermute(
        lax.slice_in_dim(latent, 0, reach, axis=1),
        "tile",
        [(j + 1, j) for j in range(tile_count - 1)],
    )
    return jnp.concatenate([from_above, latent, from_below], axis=1)


def earlier_blocks(features, depth):
    tm_count = lax.axis_size("tm")
    parts = [
        lax.ppermute(features, "tm", [(k, k + back) for k in range(tm_count - back)])
        for back in range(depth, 0, -1)
    ]
    return jnp.concatenate(parts + [features], axis=0)


def tile_total(value):
    tile_count = lax.axis_size("tile")
    step = 1
    while step < tile_count:
        value = value + lax.ppermute(
            value, "tile", [(j, j ^ step) for j in range(tile_count)]
        )
        step *= 2
    return value


def frame_statistics(own_hidden, row_total):
    frame_count = own_hidden.shape[0]
    block_index = lax.axis_index("tm")
    grouped = own_hidden.astype(jnp.float32).reshape(frame_count, -1, G, C // G)
    local = jnp.stack(
        [jnp.sum(grouped, axis=(1, 3)), jnp.sum(grouped * grouped, axis=(1, 3))]
    )
    block_sums = lax.all_gather(tile_total(local), "tm", axis=1, tiled=True)
    running = jnp.concatenate(
        [jnp.zeros((2, 2, G), jnp.float32), jnp.cumsum(block_sums, axis=1)], axis=1
    )
    window = lax.dynamic_slice_in_dim(running, block_index * frame_count, frame_count + 2, axis=1)
    frame_index = block_index * frame_count - 2 + jnp.arange(frame_count + 2, dtype=jnp.int32)
    cell_count = (
        jnp.maximum(frame_index + 1, 1) * (row_total * own_hidden.shape[2] * (C // G))
    ).astype(jnp.float32)[:, None]
    group_mean = window[0] / cell_count
    group_var = window[1] / cell_count - group_mean * group_mean
    return (group_mean, lax.rsqrt(jnp.maximum(group_var, 0.0) + 1e-05))


def normalize(features, group_mean, group_scale, group_norm_gain, group_norm_offset):
    repeat_count = features.shape[3] // group_mean.shape[1]
    mean_wide = jnp.repeat(group_mean, repeat_count, axis=1)[:, None, None, :]
    scale_wide = jnp.repeat(group_scale, repeat_count, axis=1)[:, None, None, :]
    scaled = (
        features.astype(jnp.float32) - mean_wide
    ) * scale_wide * group_norm_gain + group_norm_offset
    return jax.nn.silu(scaled)


def inside_mask(frame_count, row_count, frame_start, row_start, row_total):
    frame_index = frame_start + jnp.arange(frame_count, dtype=jnp.int32)
    row_index = row_start + jnp.arange(row_count, dtype=jnp.int32)
    frame_ok = frame_index >= 0
    row_ok = (row_index >= 0) & (row_index < row_total)
    return (frame_ok[:, None] & row_ok[None, :])[:, :, None, None]


def per_device(
    transformer_output_units,
    packed_unit_lookup,
    channel_latent_mean,
    channel_latent_deviation,
    entry_conv_weight,
    entry_conv_bias,
    group_norm_gain,
    group_norm_offset,
    residual_conv_weight,
    residual_conv_bias,
    enlarge_conv_weight,
    enlarge_conv_bias,
):
    tile_total = lax.axis_size("tile")
    unit_count = packed_unit_lookup.shape[1]
    unit_width = transformer_output_units.shape[2]
    slot_cap = 5 * unit_count // (2 * tile_total)
    targets = packed_unit_lookup[0]
    target_tile = targets // unit_count
    target_slot = targets % unit_count
    tile_match = target_tile[:, None] == jnp.arange(tile_total, dtype=jnp.int32)[None, :]
    earlier_same = jnp.cumsum(tile_match.astype(jnp.int32), axis=0) - 1
    send_rank = jnp.sum(jnp.where(tile_match, earlier_same, 0), axis=1)
    send_index = target_tile * slot_cap + send_rank
    select_dispatch = (
        jnp.arange(tile_total * slot_cap, dtype=jnp.int32)[:, None] == send_index[None, :]
    )
    send_units = jnp.dot(
        select_dispatch.astype(jnp.bfloat16),
        transformer_output_units[0],
        preferred_element_type=jnp.float32,
    ).astype(jnp.bfloat16)
    send_slots = jnp.sum(jnp.where(select_dispatch, target_slot[None, :] + 1, 0), axis=1)
    slot_lane = jnp.pad(
        send_slots.reshape(tile_total, slot_cap).astype(jnp.bfloat16),
        ((0, 0), (0, unit_width - slot_cap)),
    )
    packet = jnp.concatenate(
        [send_units.reshape(tile_total, slot_cap * unit_width), slot_lane], axis=1
    )
    got = lax.all_to_all(packet, "tile", split_axis=0, concat_axis=0, tiled=True)
    got_units = got[:, : slot_cap * unit_width].reshape(tile_total * slot_cap, unit_width)
    got_slots = got[:, slot_cap * unit_width : slot_cap * unit_width + slot_cap].astype(jnp.int32)
    choose_place = jnp.arange(1, unit_count + 1, dtype=jnp.int32)[:, None] == got_slots.reshape(
        1, -1
    )
    positioned_units = jnp.dot(
        choose_place.astype(jnp.bfloat16),
        got_units,
        preferred_element_type=jnp.float32,
    ).astype(jnp.bfloat16)
    unit_grid = positioned_units.reshape(FR_DEV, TH // 2, W // 4, 2, 2, 2, ZC)
    raw_latent = unit_grid.transpose(0, 1, 4, 2, 3, 5, 6).reshape(FR_DEV, TH, W, ZC)
    latent = (
        raw_latent.astype(jnp.float32) * channel_latent_deviation + channel_latent_mean
    ).astype(jnp.bfloat16)
    row_total = TH * tile_total
    frame_start = lax.axis_index("tm") * FR_DEV
    row_start = lax.axis_index("tile") * TH
    wide_latent = earlier_blocks(neighbour_rows(latent, 3), 2)
    hidden = causal_conv(wide_latent, entry_conv_weight, entry_conv_bias).astype(jnp.bfloat16)
    group_mean, group_scale = frame_statistics(hidden[2:, 2 : 2 + TH], row_total)
    activated = jnp.where(
        inside_mask(FR_DEV + 2, TH + 4, frame_start - 2, row_start - 2, row_total),
        normalize(hidden, group_mean, group_scale, group_norm_gain, group_norm_offset),
        0.0,
    ).astype(jnp.bfloat16)
    residual = jnp.where(
        inside_mask(FR_DEV, TH + 2, frame_start, row_start - 1, row_total),
        hidden[2:, 1 : 3 + TH].astype(jnp.float32)
        + causal_conv(activated, residual_conv_weight, residual_conv_bias),
        0.0,
    ).astype(jnp.bfloat16)
    return upsample_conv(residual, enlarge_conv_weight, enlarge_conv_bias)


def solution(mesh):
    placed = (
        P("tm", "tile", None),
        P("tm", "tile"),
        P(),
        P(),
        P(),
        P(),
        P(),
        P(),
        P(),
        P(),
        P(),
        P(),
    )
    return jax.shard_map(
        per_device,
        mesh=mesh,
        in_specs=placed,
        out_specs=P("tm", "tile", None, None),
        check_vma=False,
    )
```

```python
import jax
import jax.numpy as jnp
from jax import lax
from jax.sharding import PartitionSpec as P

C = 384
ZC = 16
G = 32
W = 160
FR_DEV = 2
TH = 4


def spatial_columns(framed, row_count, col_count, row_moves, col_moves):
    widened = jnp.pad(framed, ((0, 0), (0, 0), (1, 1), (0, 0)))
    return jnp.concatenate(
        [
            widened[
                :, 1 + row_move : 1 + row_move + row_count, 1 + col_move : 1 + col_move + col_count
            ]
            for row_move in row_moves
            for col_move in col_moves
        ],
        axis=3,
    )


def causal_conv(framed, weight, add_bias):
    result = lax.conv_general_dilated(
        framed[None],
        weight,
        window_strides=(1, 1, 1),
        padding=((0, 0), (0, 0), (1, 1)),
        dimension_numbers=("NDHWC", "DHWIO", "NDHWC"),
        preferred_element_type=jnp.float32,
    )
    return result[0] + add_bias


def phase_weights(enlarge_conv_weight):
    wide = enlarge_conv_weight.astype(jnp.float32)
    tap_groups = (((0,), (1, 2)), ((0, 1), (2,)))
    rows_a = []
    for row_phase in range(2):
        rows_b = []
        for col_phase in range(2):
            rows_u = []
            for row_off in range(2):
                rows_v = []
                for col_off in range(2):
                    total = jnp.zeros(wide.shape[2:], jnp.float32)
                    for row_tap in tap_groups[row_phase][row_off]:
                        for col_tap in tap_groups[col_phase][col_off]:
                            total = total + wide[row_tap, col_tap]
                    rows_v.append(total)
                rows_u.append(jnp.stack(rows_v))
            rows_b.append(jnp.stack(rows_u))
        rows_a.append(jnp.stack(rows_b))
    return jnp.stack(rows_a).astype(jnp.bfloat16)


def upsample_conv(framed, enlarge_conv_weight, enlarge_conv_bias):
    frame_count = framed.shape[0]
    row_count = framed.shape[1] - 2
    col_count = framed.shape[2]
    channels = framed.shape[3]
    out_channels = enlarge_conv_weight.shape[2]
    phase_weight = phase_weights(enlarge_conv_weight)
    row_phases = []
    for row_phase in range(2):
        halves = []
        for col_phase in range(2):
            row_moves = [row_phase - 1 + row_off for row_off in range(2)]
            col_moves = [col_phase - 1 + col_off for col_off in range(2)]
            columns = spatial_columns(framed, row_count, col_count, row_moves, col_moves)
            flat_weight = (
                phase_weight[row_phase, col_phase]
                .transpose(0, 1, 3, 2)
                .reshape(4 * channels, out_channels)
            )
            halves.append(
                jnp.dot(columns, flat_weight, preferred_element_type=jnp.float32)
                + enlarge_conv_bias
            )
        row_phases.append(jnp.concatenate(halves, axis=3).astype(jnp.bfloat16))
    return jnp.stack(row_phases, axis=2).reshape(
        frame_count, 2 * row_count, col_count, 2 * out_channels
    )


def neighbour_rows(latent, reach):
    tile_count = lax.axis_size("tile")
    rows = latent.shape[1]
    from_above = lax.ppermute(
        lax.slice_in_dim(latent, rows - reach, rows, axis=1),
        "tile",
        [(j, j + 1) for j in range(tile_count - 1)],
    )
    from_below = lax.ppermute(
        lax.slice_in_dim(latent, 0, reach, axis=1),
        "tile",
        [(j + 1, j) for j in range(tile_count - 1)],
    )
    return jnp.concatenate([from_above, latent, from_below], axis=1)


def earlier_blocks(features, depth):
    tm_count = lax.axis_size("tm")
    parts = [
        lax.ppermute(features, "tm", [(k, k + back) for k in range(tm_count - back)])
        for back in range(depth, 0, -1)
    ]
    return jnp.concatenate(parts + [features], axis=0)


def frame_statistics(own_hidden, row_total):
    frame_count = own_hidden.shape[0]
    block_total = lax.axis_size("tm")
    tile_count = lax.axis_size("tile")
    block_index = lax.axis_index("tm")
    grouped = own_hidden.astype(jnp.float32).reshape(frame_count, -1, G, C // G)
    local = jnp.stack(
        [jnp.sum(grouped, axis=(1, 3)), jnp.sum(grouped * grouped, axis=(1, 3))]
    ).reshape(1, -1)
    spread = jnp.broadcast_to(local, (block_total * tile_count, local.shape[1]))
    gathered = lax.all_to_all(spread, ("tm", "tile"), 0, 0, tiled=True)
    block_sums = jnp.sum(gathered.reshape(block_total, tile_count, 2, frame_count, G), axis=1)
    frame_sums = block_sums.transpose(1, 0, 2, 3).reshape(2, block_total * frame_count, G)
    running = jnp.concatenate(
        [jnp.zeros((2, 2, G), jnp.float32), jnp.cumsum(frame_sums, axis=1)], axis=1
    )
    window = lax.dynamic_slice_in_dim(running, block_index * frame_count, frame_count + 2, axis=1)
    frame_index = block_index * frame_count - 2 + jnp.arange(frame_count + 2, dtype=jnp.int32)
    cell_count = (
        jnp.maximum(frame_index + 1, 1) * (row_total * own_hidden.shape[2] * (C // G))
    ).astype(jnp.float32)[:, None]
    group_mean = window[0] / cell_count
    group_var = window[1] / cell_count - group_mean * group_mean
    return (group_mean, lax.rsqrt(jnp.maximum(group_var, 0.0) + 1e-05))


def normalize(features, group_mean, group_scale, group_norm_gain, group_norm_offset):
    repeat_count = features.shape[3] // group_mean.shape[1]
    mean_wide = jnp.repeat(group_mean, repeat_count, axis=1)[:, None, None, :]
    scale_wide = jnp.repeat(group_scale, repeat_count, axis=1)[:, None, None, :]
    scaled = (
        features.astype(jnp.float32) - mean_wide
    ) * scale_wide * group_norm_gain + group_norm_offset
    return jax.nn.silu(scaled)


def inside_mask(frame_count, row_count, frame_start, row_start, row_total):
    frame_index = frame_start + jnp.arange(frame_count, dtype=jnp.int32)
    row_index = row_start + jnp.arange(row_count, dtype=jnp.int32)
    frame_ok = frame_index >= 0
    row_ok = (row_index >= 0) & (row_index < row_total)
    return (frame_ok[:, None] & row_ok[None, :])[:, :, None, None]


def per_device(
    transformer_output_units,
    packed_unit_lookup,
    channel_latent_mean,
    channel_latent_deviation,
    entry_conv_weight,
    entry_conv_bias,
    group_norm_gain,
    group_norm_offset,
    residual_conv_weight,
    residual_conv_bias,
    enlarge_conv_weight,
    enlarge_conv_bias,
):
    tile_total = lax.axis_size("tile")
    unit_count = packed_unit_lookup.shape[1]
    unit_width = transformer_output_units.shape[2]
    slot_cap = 5 * unit_count // (2 * tile_total)
    targets = packed_unit_lookup[0]
    target_tile = targets // unit_count
    target_slot = targets % unit_count
    tile_match = target_tile[:, None] == jnp.arange(tile_total, dtype=jnp.int32)[None, :]
    earlier_same = jnp.cumsum(tile_match.astype(jnp.int32), axis=0) - 1
    send_rank = jnp.sum(jnp.where(tile_match, earlier_same, 0), axis=1)
    send_index = target_tile * slot_cap + send_rank
    select_dispatch = (
        jnp.arange(tile_total * slot_cap, dtype=jnp.int32)[:, None] == send_index[None, :]
    )
    send_units = jnp.dot(
        select_dispatch.astype(jnp.bfloat16),
        transformer_output_units[0],
        preferred_element_type=jnp.float32,
    ).astype(jnp.bfloat16)
    send_slots = jnp.sum(jnp.where(select_dispatch, target_slot[None, :] + 1, 0), axis=1)
    slot_lane = jnp.pad(
        send_slots.reshape(tile_total, slot_cap).astype(jnp.bfloat16),
        ((0, 0), (0, unit_width - slot_cap)),
    )
    packet = jnp.concatenate(
        [send_units.reshape(tile_total, slot_cap * unit_width), slot_lane], axis=1
    )
    got = lax.all_to_all(packet, "tile", split_axis=0, concat_axis=0, tiled=True)
    got_units = got[:, : slot_cap * unit_width].reshape(tile_total * slot_cap, unit_width)
    got_slots = got[:, slot_cap * unit_width : slot_cap * unit_width + slot_cap].astype(jnp.int32)
    choose_place = jnp.arange(1, unit_count + 1, dtype=jnp.int32)[:, None] == got_slots.reshape(
        1, -1
    )
    positioned_units = jnp.dot(
        choose_place.astype(jnp.bfloat16),
        got_units,
        preferred_element_type=jnp.float32,
    ).astype(jnp.bfloat16)
    unit_grid = positioned_units.reshape(FR_DEV, TH // 2, W // 4, 2, 2, 2, ZC)
    raw_latent = unit_grid.transpose(0, 1, 4, 2, 3, 5, 6).reshape(FR_DEV, TH, W, ZC)
    latent = (
        raw_latent.astype(jnp.float32) * channel_latent_deviation + channel_latent_mean
    ).astype(jnp.bfloat16)
    row_total = TH * tile_total
    frame_start = lax.axis_index("tm") * FR_DEV
    row_start = lax.axis_index("tile") * TH
    wide_latent = earlier_blocks(neighbour_rows(latent, 3), 2)
    hidden = causal_conv(wide_latent, entry_conv_weight, entry_conv_bias).astype(jnp.bfloat16)
    group_mean, group_scale = frame_statistics(hidden[2:, 2 : 2 + TH], row_total)
    activated = jnp.where(
        inside_mask(FR_DEV + 2, TH + 4, frame_start - 2, row_start - 2, row_total),
        normalize(hidden, group_mean, group_scale, group_norm_gain, group_norm_offset),
        0.0,
    ).astype(jnp.bfloat16)
    residual = jnp.where(
        inside_mask(FR_DEV, TH + 2, frame_start, row_start - 1, row_total),
        hidden[2:, 1 : 3 + TH].astype(jnp.float32)
        + causal_conv(activated, residual_conv_weight, residual_conv_bias),
        0.0,
    ).astype(jnp.bfloat16)
    return upsample_conv(residual, enlarge_conv_weight, enlarge_conv_bias)


def solution(mesh):
    placed = (
        P("tm", "tile", None),
        P("tm", "tile"),
        P(),
        P(),
        P(),
        P(),
        P(),
        P(),
        P(),
        P(),
        P(),
        P(),
    )
    return jax.shard_map(
        per_device,
        mesh=mesh,
        in_specs=placed,
        out_specs=P("tm", "tile", None, None),
        check_vma=False,
    )
```

```python
import jax
import jax.numpy as jnp
from jax import lax
from jax.sharding import PartitionSpec as P

C = 384
ZC = 16
G = 32
W = 160
FR_DEV = 2
TH = 4


def spatial_columns(framed, row_count, col_count, row_moves, col_moves):
    widened = jnp.pad(framed, ((0, 0), (0, 0), (1, 1), (0, 0)))
    return jnp.concatenate(
        [
            widened[
                :, 1 + row_move : 1 + row_move + row_count, 1 + col_move : 1 + col_move + col_count
            ]
            for row_move in row_moves
            for col_move in col_moves
        ],
        axis=3,
    )


def causal_conv(framed, weight, add_bias):
    frame_count = framed.shape[0] - 2
    row_count = framed.shape[1] - 2
    col_count = framed.shape[2]
    columns = spatial_columns(framed, row_count, col_count, (-1, 0, 1), (-1, 0, 1))
    flat_weight = weight.reshape(3, -1, weight.shape[-1])
    running = None
    for time_tap in range(3):
        tap_term = jnp.dot(
            columns[time_tap : time_tap + frame_count],
            flat_weight[time_tap],
            preferred_element_type=jnp.float32,
        )
        running = tap_term if running is None else running + tap_term
    return running + add_bias


def phase_weights(enlarge_conv_weight):
    wide = enlarge_conv_weight.astype(jnp.float32)
    tap_groups = (((0,), (1, 2)), ((0, 1), (2,)))
    rows_a = []
    for row_phase in range(2):
        rows_b = []
        for col_phase in range(2):
            rows_u = []
            for row_off in range(2):
                rows_v = []
                for col_off in range(2):
                    total = jnp.zeros(wide.shape[2:], jnp.float32)
                    for row_tap in tap_groups[row_phase][row_off]:
                        for col_tap in tap_groups[col_phase][col_off]:
                            total = total + wide[row_tap, col_tap]
                    rows_v.append(total)
                rows_u.append(jnp.stack(rows_v))
            rows_b.append(jnp.stack(rows_u))
        rows_a.append(jnp.stack(rows_b))
    return jnp.stack(rows_a).astype(jnp.bfloat16)


def upsample_conv(framed, enlarge_conv_weight, enlarge_conv_bias):
    frame_count = framed.shape[0]
    row_count = framed.shape[1] - 2
    col_count = framed.shape[2]
    channels = framed.shape[3]
    out_channels = enlarge_conv_weight.shape[2]
    phase_weight = phase_weights(enlarge_conv_weight)
    row_phases = []
    for row_phase in range(2):
        halves = []
        for col_phase in range(2):
            row_moves = [row_phase - 1 + row_off for row_off in range(2)]
            col_moves = [col_phase - 1 + col_off for col_off in range(2)]
            columns = spatial_columns(framed, row_count, col_count, row_moves, col_moves)
            flat_weight = (
                phase_weight[row_phase, col_phase]
                .transpose(0, 1, 3, 2)
                .reshape(4 * channels, out_channels)
            )
            halves.append(
                jnp.dot(columns, flat_weight, preferred_element_type=jnp.float32)
                + enlarge_conv_bias
            )
        row_phases.append(jnp.concatenate(halves, axis=3).astype(jnp.bfloat16))
    return jnp.stack(row_phases, axis=2).reshape(
        frame_count, 2 * row_count, col_count, 2 * out_channels
    )


def neighbour_rows(latent, reach):
    tile_count = lax.axis_size("tile")
    rows = latent.shape[1]
    from_above = lax.ppermute(
        lax.slice_in_dim(latent, rows - reach, rows, axis=1),
        "tile",
        [(j, j + 1) for j in range(tile_count - 1)],
    )
    from_below = lax.ppermute(
        lax.slice_in_dim(latent, 0, reach, axis=1),
        "tile",
        [(j + 1, j) for j in range(tile_count - 1)],
    )
    return jnp.concatenate([from_above, latent, from_below], axis=1)


def earlier_blocks(features, depth):
    tm_count = lax.axis_size("tm")
    parts = [
        lax.ppermute(features, "tm", [(k, k + back) for k in range(tm_count - back)])
        for back in range(depth, 0, -1)
    ]
    return jnp.concatenate(parts + [features], axis=0)


def frame_statistics(own_hidden, row_total):
    frame_count = own_hidden.shape[0]
    block_total = lax.axis_size("tm")
    tile_count = lax.axis_size("tile")
    block_index = lax.axis_index("tm")
    grouped = own_hidden.astype(jnp.float32).reshape(frame_count, -1, G, C // G)
    local = jnp.stack(
        [jnp.sum(grouped, axis=(1, 3)), jnp.sum(grouped * grouped, axis=(1, 3))]
    ).reshape(1, -1)
    spread = jnp.broadcast_to(local, (block_total * tile_count, local.shape[1]))
    gathered = lax.all_to_all(spread, ("tm", "tile"), 0, 0, tiled=True)
    block_sums = jnp.sum(gathered.reshape(block_total, tile_count, 2, frame_count, G), axis=1)
    frame_sums = block_sums.transpose(1, 0, 2, 3).reshape(2, block_total * frame_count, G)
    running = jnp.concatenate(
        [jnp.zeros((2, 2, G), jnp.float32), jnp.cumsum(frame_sums, axis=1)], axis=1
    )
    window = lax.dynamic_slice_in_dim(running, block_index * frame_count, frame_count + 2, axis=1)
    frame_index = block_index * frame_count - 2 + jnp.arange(frame_count + 2, dtype=jnp.int32)
    cell_count = (
        jnp.maximum(frame_index + 1, 1) * (row_total * own_hidden.shape[2] * (C // G))
    ).astype(jnp.float32)[:, None]
    group_mean = window[0] / cell_count
    group_var = window[1] / cell_count - group_mean * group_mean
    return (group_mean, lax.rsqrt(jnp.maximum(group_var, 0.0) + 1e-05))


def normalize(features, group_mean, group_scale, group_norm_gain, group_norm_offset):
    repeat_count = features.shape[3] // group_mean.shape[1]
    mean_wide = jnp.repeat(group_mean, repeat_count, axis=1)[:, None, None, :]
    scale_wide = jnp.repeat(group_scale, repeat_count, axis=1)[:, None, None, :]
    scaled = (
        features.astype(jnp.float32) - mean_wide
    ) * scale_wide * group_norm_gain + group_norm_offset
    return jax.nn.silu(scaled)


def inside_mask(frame_count, row_count, frame_start, row_start, row_total):
    frame_index = frame_start + jnp.arange(frame_count, dtype=jnp.int32)
    row_index = row_start + jnp.arange(row_count, dtype=jnp.int32)
    frame_ok = frame_index >= 0
    row_ok = (row_index >= 0) & (row_index < row_total)
    return (frame_ok[:, None] & row_ok[None, :])[:, :, None, None]


def per_device(
    transformer_output_units,
    packed_unit_lookup,
    channel_latent_mean,
    channel_latent_deviation,
    entry_conv_weight,
    entry_conv_bias,
    group_norm_gain,
    group_norm_offset,
    residual_conv_weight,
    residual_conv_bias,
    enlarge_conv_weight,
    enlarge_conv_bias,
):
    tile_total = lax.axis_size("tile")
    unit_count = packed_unit_lookup.shape[1]
    unit_width = transformer_output_units.shape[2]
    slot_cap = 5 * unit_count // (2 * tile_total)
    targets = packed_unit_lookup[0]
    target_tile = targets // unit_count
    target_slot = targets % unit_count
    tile_match = target_tile[:, None] == jnp.arange(tile_total, dtype=jnp.int32)[None, :]
    earlier_same = jnp.cumsum(tile_match.astype(jnp.int32), axis=0) - 1
    send_rank = jnp.sum(jnp.where(tile_match, earlier_same, 0), axis=1)
    send_index = target_tile * slot_cap + send_rank
    select_dispatch = (
        jnp.arange(tile_total * slot_cap, dtype=jnp.int32)[:, None] == send_index[None, :]
    )
    send_units = jnp.dot(
        select_dispatch.astype(jnp.bfloat16),
        transformer_output_units[0],
        preferred_element_type=jnp.float32,
    ).astype(jnp.bfloat16)
    send_slots = jnp.sum(jnp.where(select_dispatch, target_slot[None, :] + 1, 0), axis=1)
    slot_lane = jnp.pad(
        send_slots.reshape(tile_total, slot_cap).astype(jnp.bfloat16),
        ((0, 0), (0, unit_width - slot_cap)),
    )
    packet = jnp.concatenate(
        [send_units.reshape(tile_total, slot_cap * unit_width), slot_lane], axis=1
    )
    got = lax.all_to_all(packet, "tile", split_axis=0, concat_axis=0, tiled=True)
    got_units = got[:, : slot_cap * unit_width].reshape(tile_total * slot_cap, unit_width)
    got_slots = got[:, slot_cap * unit_width : slot_cap * unit_width + slot_cap].astype(jnp.int32)
    choose_place = jnp.arange(1, unit_count + 1, dtype=jnp.int32)[:, None] == got_slots.reshape(
        1, -1
    )
    positioned_units = jnp.dot(
        choose_place.astype(jnp.bfloat16),
        got_units,
        preferred_element_type=jnp.float32,
    ).astype(jnp.bfloat16)
    unit_grid = positioned_units.reshape(FR_DEV, TH // 2, W // 4, 2, 2, 2, ZC)
    raw_latent = unit_grid.transpose(0, 1, 4, 2, 3, 5, 6).reshape(FR_DEV, TH, W, ZC)
    latent = (
        raw_latent.astype(jnp.float32) * channel_latent_deviation + channel_latent_mean
    ).astype(jnp.bfloat16)
    row_total = TH * tile_total
    frame_start = lax.axis_index("tm") * FR_DEV
    row_start = lax.axis_index("tile") * TH
    wide_latent = earlier_blocks(neighbour_rows(latent, 3), 2)
    hidden = causal_conv(wide_latent, entry_conv_weight, entry_conv_bias).astype(jnp.bfloat16)
    group_mean, group_scale = frame_statistics(hidden[2:, 2 : 2 + TH], row_total)
    activated = jnp.where(
        inside_mask(FR_DEV + 2, TH + 4, frame_start - 2, row_start - 2, row_total),
        normalize(hidden, group_mean, group_scale, group_norm_gain, group_norm_offset),
        0.0,
    ).astype(jnp.bfloat16)
    residual = jnp.where(
        inside_mask(FR_DEV, TH + 2, frame_start, row_start - 1, row_total),
        hidden[2:, 1 : 3 + TH].astype(jnp.float32)
        + causal_conv(activated, residual_conv_weight, residual_conv_bias),
        0.0,
    ).astype(jnp.bfloat16)
    return upsample_conv(residual, enlarge_conv_weight, enlarge_conv_bias)


def solution(mesh):
    placed = (
        P("tm", "tile", None),
        P("tm", "tile"),
        P(),
        P(),
        P(),
        P(),
        P(),
        P(),
        P(),
        P(),
        P(),
        P(),
    )
    return jax.shard_map(
        per_device,
        mesh=mesh,
        in_specs=placed,
        out_specs=P("tm", "tile", None, None),
        check_vma=False,
    )
```

```python
import jax
import jax.numpy as jnp
from jax import lax
from jax.sharding import PartitionSpec as P

C = 384
ZC = 16
G = 32
W = 160
FR_DEV = 2
TH = 4


def spatial_columns(framed, row_count, col_count, row_moves, col_moves):
    widened = jnp.pad(framed, ((0, 0), (0, 0), (1, 1), (0, 0)))
    return jnp.concatenate(
        [
            widened[
                :, 1 + row_move : 1 + row_move + row_count, 1 + col_move : 1 + col_move + col_count
            ]
            for row_move in row_moves
            for col_move in col_moves
        ],
        axis=3,
    )


def causal_conv(framed, weight, add_bias):
    frame_count = framed.shape[0] - 2
    row_count = framed.shape[1] - 2
    col_count = framed.shape[2]
    columns = spatial_columns(framed, row_count, col_count, (-1, 0, 1), (-1, 0, 1))
    flat_weight = weight.reshape(3, -1, weight.shape[-1])
    running = None
    for time_tap in range(3):
        tap_term = jnp.dot(
            columns[time_tap : time_tap + frame_count],
            flat_weight[time_tap],
            preferred_element_type=jnp.float32,
        )
        running = tap_term if running is None else running + tap_term
    return running + add_bias


def native_causal_conv(framed, weight, add_bias):
    result = lax.conv_general_dilated(
        framed[None],
        weight,
        window_strides=(1, 1, 1),
        padding=((0, 0), (0, 0), (1, 1)),
        dimension_numbers=("NDHWC", "DHWIO", "NDHWC"),
        preferred_element_type=jnp.float32,
    )
    return result[0] + add_bias


def phase_weights(enlarge_conv_weight):
    wide = enlarge_conv_weight.astype(jnp.float32)
    tap_groups = (((0,), (1, 2)), ((0, 1), (2,)))
    rows_a = []
    for row_phase in range(2):
        rows_b = []
        for col_phase in range(2):
            rows_u = []
            for row_off in range(2):
                rows_v = []
                for col_off in range(2):
                    total = jnp.zeros(wide.shape[2:], jnp.float32)
                    for row_tap in tap_groups[row_phase][row_off]:
                        for col_tap in tap_groups[col_phase][col_off]:
                            total = total + wide[row_tap, col_tap]
                    rows_v.append(total)
                rows_u.append(jnp.stack(rows_v))
            rows_b.append(jnp.stack(rows_u))
        rows_a.append(jnp.stack(rows_b))
    return jnp.stack(rows_a).astype(jnp.bfloat16)


def upsample_conv(framed, enlarge_conv_weight, enlarge_conv_bias):
    frame_count = framed.shape[0]
    row_count = framed.shape[1] - 2
    col_count = framed.shape[2]
    channels = framed.shape[3]
    out_channels = enlarge_conv_weight.shape[2]
    phase_weight = phase_weights(enlarge_conv_weight)
    row_phases = []
    for row_phase in range(2):
        halves = []
        for col_phase in range(2):
            row_moves = [row_phase - 1 + row_off for row_off in range(2)]
            col_moves = [col_phase - 1 + col_off for col_off in range(2)]
            columns = spatial_columns(framed, row_count, col_count, row_moves, col_moves)
            flat_weight = (
                phase_weight[row_phase, col_phase]
                .transpose(0, 1, 3, 2)
                .reshape(4 * channels, out_channels)
            )
            halves.append(
                jnp.dot(columns, flat_weight, preferred_element_type=jnp.float32)
                + enlarge_conv_bias
            )
        row_phases.append(jnp.concatenate(halves, axis=3).astype(jnp.bfloat16))
    return jnp.stack(row_phases, axis=2).reshape(
        frame_count, 2 * row_count, col_count, 2 * out_channels
    )


def neighbour_rows(latent, reach):
    tile_count = lax.axis_size("tile")
    rows = latent.shape[1]
    from_above = lax.ppermute(
        lax.slice_in_dim(latent, rows - reach, rows, axis=1),
        "tile",
        [(j, j + 1) for j in range(tile_count - 1)],
    )
    from_below = lax.ppermute(
        lax.slice_in_dim(latent, 0, reach, axis=1),
        "tile",
        [(j + 1, j) for j in range(tile_count - 1)],
    )
    return jnp.concatenate([from_above, latent, from_below], axis=1)


def earlier_blocks(features, depth):
    tm_count = lax.axis_size("tm")
    parts = [
        lax.ppermute(features, "tm", [(k, k + back) for k in range(tm_count - back)])
        for back in range(depth, 0, -1)
    ]
    return jnp.concatenate(parts + [features], axis=0)


def frame_statistics(own_hidden, row_total):
    frame_count = own_hidden.shape[0]
    block_total = lax.axis_size("tm")
    tile_count = lax.axis_size("tile")
    block_index = lax.axis_index("tm")
    grouped = own_hidden.astype(jnp.float32).reshape(frame_count, -1, G, C // G)
    local = jnp.stack(
        [jnp.sum(grouped, axis=(1, 3)), jnp.sum(grouped * grouped, axis=(1, 3))]
    ).reshape(1, -1)
    spread = jnp.broadcast_to(local, (block_total * tile_count, local.shape[1]))
    gathered = lax.all_to_all(spread, ("tm", "tile"), 0, 0, tiled=True)
    block_sums = jnp.sum(gathered.reshape(block_total, tile_count, 2, frame_count, G), axis=1)
    frame_sums = block_sums.transpose(1, 0, 2, 3).reshape(2, block_total * frame_count, G)
    running = jnp.concatenate(
        [jnp.zeros((2, 2, G), jnp.float32), jnp.cumsum(frame_sums, axis=1)], axis=1
    )
    window = lax.dynamic_slice_in_dim(running, block_index * frame_count, frame_count + 2, axis=1)
    frame_index = block_index * frame_count - 2 + jnp.arange(frame_count + 2, dtype=jnp.int32)
    cell_count = (
        jnp.maximum(frame_index + 1, 1) * (row_total * own_hidden.shape[2] * (C // G))
    ).astype(jnp.float32)[:, None]
    group_mean = window[0] / cell_count
    group_var = window[1] / cell_count - group_mean * group_mean
    return (group_mean, lax.rsqrt(jnp.maximum(group_var, 0.0) + 1e-05))


def normalize(features, group_mean, group_scale, group_norm_gain, group_norm_offset):
    repeat_count = features.shape[3] // group_mean.shape[1]
    mean_wide = jnp.repeat(group_mean, repeat_count, axis=1)[:, None, None, :]
    scale_wide = jnp.repeat(group_scale, repeat_count, axis=1)[:, None, None, :]
    scaled = (
        features.astype(jnp.float32) - mean_wide
    ) * scale_wide * group_norm_gain + group_norm_offset
    return jax.nn.silu(scaled)


def inside_mask(frame_count, row_count, frame_start, row_start, row_total):
    frame_index = frame_start + jnp.arange(frame_count, dtype=jnp.int32)
    row_index = row_start + jnp.arange(row_count, dtype=jnp.int32)
    frame_ok = frame_index >= 0
    row_ok = (row_index >= 0) & (row_index < row_total)
    return (frame_ok[:, None] & row_ok[None, :])[:, :, None, None]


def per_device(
    transformer_output_units,
    packed_unit_lookup,
    channel_latent_mean,
    channel_latent_deviation,
    entry_conv_weight,
    entry_conv_bias,
    group_norm_gain,
    group_norm_offset,
    residual_conv_weight,
    residual_conv_bias,
    enlarge_conv_weight,
    enlarge_conv_bias,
):
    tile_total = lax.axis_size("tile")
    unit_count = packed_unit_lookup.shape[1]
    unit_width = transformer_output_units.shape[2]
    slot_cap = 5 * unit_count // (2 * tile_total)
    targets = packed_unit_lookup[0]
    target_tile = targets // unit_count
    target_slot = targets % unit_count
    tile_match = target_tile[:, None] == jnp.arange(tile_total, dtype=jnp.int32)[None, :]
    earlier_same = jnp.cumsum(tile_match.astype(jnp.int32), axis=0) - 1
    send_rank = jnp.sum(jnp.where(tile_match, earlier_same, 0), axis=1)
    send_index = target_tile * slot_cap + send_rank
    select_dispatch = (
        jnp.arange(tile_total * slot_cap, dtype=jnp.int32)[:, None] == send_index[None, :]
    )
    send_units = jnp.dot(
        select_dispatch.astype(jnp.bfloat16),
        transformer_output_units[0],
        preferred_element_type=jnp.float32,
    ).astype(jnp.bfloat16)
    send_slots = jnp.sum(jnp.where(select_dispatch, target_slot[None, :] + 1, 0), axis=1)
    slot_lane = jnp.pad(
        send_slots.reshape(tile_total, slot_cap).astype(jnp.bfloat16),
        ((0, 0), (0, unit_width - slot_cap)),
    )
    packet = jnp.concatenate(
        [send_units.reshape(tile_total, slot_cap * unit_width), slot_lane], axis=1
    )
    got = lax.all_to_all(packet, "tile", split_axis=0, concat_axis=0, tiled=True)
    got_units = got[:, : slot_cap * unit_width].reshape(tile_total * slot_cap, unit_width)
    got_slots = got[:, slot_cap * unit_width : slot_cap * unit_width + slot_cap].astype(jnp.int32)
    choose_place = jnp.arange(1, unit_count + 1, dtype=jnp.int32)[:, None] == got_slots.reshape(
        1, -1
    )
    positioned_units = jnp.dot(
        choose_place.astype(jnp.bfloat16),
        got_units,
        preferred_element_type=jnp.float32,
    ).astype(jnp.bfloat16)
    unit_grid = positioned_units.reshape(FR_DEV, TH // 2, W // 4, 2, 2, 2, ZC)
    raw_latent = unit_grid.transpose(0, 1, 4, 2, 3, 5, 6).reshape(FR_DEV, TH, W, ZC)
    latent = (
        raw_latent.astype(jnp.float32) * channel_latent_deviation + channel_latent_mean
    ).astype(jnp.bfloat16)
    row_total = TH * tile_total
    frame_start = lax.axis_index("tm") * FR_DEV
    row_start = lax.axis_index("tile") * TH
    wide_latent = earlier_blocks(neighbour_rows(latent, 3), 2)
    hidden = causal_conv(wide_latent, entry_conv_weight, entry_conv_bias).astype(jnp.bfloat16)
    group_mean, group_scale = frame_statistics(hidden[2:, 2 : 2 + TH], row_total)
    activated = jnp.where(
        inside_mask(FR_DEV + 2, TH + 4, frame_start - 2, row_start - 2, row_total),
        normalize(hidden, group_mean, group_scale, group_norm_gain, group_norm_offset),
        0.0,
    ).astype(jnp.bfloat16)
    residual = jnp.where(
        inside_mask(FR_DEV, TH + 2, frame_start, row_start - 1, row_total),
        hidden[2:, 1 : 3 + TH].astype(jnp.float32)
        + native_causal_conv(activated, residual_conv_weight, residual_conv_bias),
        0.0,
    ).astype(jnp.bfloat16)
    return upsample_conv(residual, enlarge_conv_weight, enlarge_conv_bias)


def solution(mesh):
    placed = (
        P("tm", "tile", None),
        P("tm", "tile"),
        P(),
        P(),
        P(),
        P(),
        P(),
        P(),
        P(),
        P(),
        P(),
        P(),
    )
    return jax.shard_map(
        per_device,
        mesh=mesh,
        in_specs=placed,
        out_specs=P("tm", "tile", None, None),
        check_vma=False,
    )
```

```python
import jax
import jax.numpy as jnp
from jax import lax
from jax.sharding import PartitionSpec as P

C = 384
ZC = 16
G = 32
W = 160
FR_DEV = 2
TH = 4


def spatial_columns(framed, row_count, col_count, row_moves, col_moves):
    widened = jnp.pad(framed, ((0, 0), (0, 0), (1, 1), (0, 0)))
    return jnp.concatenate(
        [
            widened[
                :, 1 + row_move : 1 + row_move + row_count, 1 + col_move : 1 + col_move + col_count
            ]
            for row_move in row_moves
            for col_move in col_moves
        ],
        axis=3,
    )


def causal_conv(framed, weight, add_bias):
    frame_count = framed.shape[0] - 2
    row_count = framed.shape[1] - 2
    col_count = framed.shape[2]
    columns = spatial_columns(framed, row_count, col_count, (-1, 0, 1), (-1, 0, 1))
    flat_weight = weight.reshape(3, -1, weight.shape[-1])
    running = None
    for time_tap in range(3):
        tap_term = jnp.dot(
            columns[time_tap : time_tap + frame_count],
            flat_weight[time_tap],
            preferred_element_type=jnp.float32,
        )
        running = tap_term if running is None else running + tap_term
    return running + add_bias


def native_causal_conv(framed, weight, add_bias):
    result = lax.conv_general_dilated(
        framed[None],
        weight,
        window_strides=(1, 1, 1),
        padding=((0, 0), (0, 0), (1, 1)),
        dimension_numbers=("NDHWC", "DHWIO", "NDHWC"),
        preferred_element_type=jnp.float32,
    )
    return result[0] + add_bias


def phase_weights(enlarge_conv_weight):
    wide = enlarge_conv_weight.astype(jnp.float32)
    tap_groups = (((0,), (1, 2)), ((0, 1), (2,)))
    rows_a = []
    for row_phase in range(2):
        rows_b = []
        for col_phase in range(2):
            rows_u = []
            for row_off in range(2):
                rows_v = []
                for col_off in range(2):
                    total = jnp.zeros(wide.shape[2:], jnp.float32)
                    for row_tap in tap_groups[row_phase][row_off]:
                        for col_tap in tap_groups[col_phase][col_off]:
                            total = total + wide[row_tap, col_tap]
                    rows_v.append(total)
                rows_u.append(jnp.stack(rows_v))
            rows_b.append(jnp.stack(rows_u))
        rows_a.append(jnp.stack(rows_b))
    return jnp.stack(rows_a).astype(jnp.bfloat16)


def upsample_conv(framed, enlarge_conv_weight, enlarge_conv_bias):
    frame_count = framed.shape[0]
    row_count = framed.shape[1] - 2
    col_count = framed.shape[2]
    out_channels = enlarge_conv_weight.shape[2]
    phase_weight = phase_weights(enlarge_conv_weight)
    empty = jnp.zeros(phase_weight.shape[4:], phase_weight.dtype)
    both_bias = jnp.concatenate([enlarge_conv_bias, enlarge_conv_bias])
    row_phases = []
    for row_phase in range(2):
        kernel = jnp.stack(
            [
                jnp.stack(
                    [
                        jnp.concatenate(
                            [
                                phase_weight[row_phase, col_phase, row_off, col_tap - col_phase]
                                if 0 <= col_tap - col_phase <= 1
                                else empty
                                for col_phase in range(2)
                            ],
                            axis=0,
                        )
                        for col_tap in range(3)
                    ]
                )
                for row_off in range(2)
            ]
        )
        result = lax.conv_general_dilated(
            framed[:, row_phase : row_phase + row_count + 1],
            kernel,
            window_strides=(1, 1),
            padding=((0, 0), (1, 1)),
            dimension_numbers=("NHWC", "HWOI", "NHWC"),
            preferred_element_type=jnp.float32,
        )
        row_phases.append((result + both_bias).astype(jnp.bfloat16))
    return jnp.stack(row_phases, axis=2).reshape(
        frame_count, 2 * row_count, col_count, 2 * out_channels
    )


def neighbour_rows(latent, reach):
    tile_count = lax.axis_size("tile")
    rows = latent.shape[1]
    from_above = lax.ppermute(
        lax.slice_in_dim(latent, rows - reach, rows, axis=1),
        "tile",
        [(j, j + 1) for j in range(tile_count - 1)],
    )
    from_below = lax.ppermute(
        lax.slice_in_dim(latent, 0, reach, axis=1),
        "tile",
        [(j + 1, j) for j in range(tile_count - 1)],
    )
    return jnp.concatenate([from_above, latent, from_below], axis=1)


def earlier_blocks(features, depth):
    tm_count = lax.axis_size("tm")
    parts = [
        lax.ppermute(features, "tm", [(k, k + back) for k in range(tm_count - back)])
        for back in range(depth, 0, -1)
    ]
    return jnp.concatenate(parts + [features], axis=0)


def frame_statistics(own_hidden, row_total):
    frame_count = own_hidden.shape[0]
    block_total = lax.axis_size("tm")
    tile_count = lax.axis_size("tile")
    block_index = lax.axis_index("tm")
    grouped = own_hidden.astype(jnp.float32).reshape(frame_count, -1, G, C // G)
    local = jnp.stack(
        [jnp.sum(grouped, axis=(1, 3)), jnp.sum(grouped * grouped, axis=(1, 3))]
    ).reshape(1, -1)
    spread = jnp.broadcast_to(local, (block_total * tile_count, local.shape[1]))
    gathered = lax.all_to_all(spread, ("tm", "tile"), 0, 0, tiled=True)
    block_sums = jnp.sum(gathered.reshape(block_total, tile_count, 2, frame_count, G), axis=1)
    frame_sums = block_sums.transpose(1, 0, 2, 3).reshape(2, block_total * frame_count, G)
    running = jnp.concatenate(
        [jnp.zeros((2, 2, G), jnp.float32), jnp.cumsum(frame_sums, axis=1)], axis=1
    )
    window = lax.dynamic_slice_in_dim(running, block_index * frame_count, frame_count + 2, axis=1)
    frame_index = block_index * frame_count - 2 + jnp.arange(frame_count + 2, dtype=jnp.int32)
    cell_count = (
        jnp.maximum(frame_index + 1, 1) * (row_total * own_hidden.shape[2] * (C // G))
    ).astype(jnp.float32)[:, None]
    group_mean = window[0] / cell_count
    group_var = window[1] / cell_count - group_mean * group_mean
    return (group_mean, lax.rsqrt(jnp.maximum(group_var, 0.0) + 1e-05))


def normalize(features, group_mean, group_scale, group_norm_gain, group_norm_offset):
    repeat_count = features.shape[3] // group_mean.shape[1]
    mean_wide = jnp.repeat(group_mean, repeat_count, axis=1)[:, None, None, :]
    scale_wide = jnp.repeat(group_scale, repeat_count, axis=1)[:, None, None, :]
    scaled = (
        features.astype(jnp.float32) - mean_wide
    ) * scale_wide * group_norm_gain + group_norm_offset
    return jax.nn.silu(scaled)


def inside_mask(frame_count, row_count, frame_start, row_start, row_total):
    frame_index = frame_start + jnp.arange(frame_count, dtype=jnp.int32)
    row_index = row_start + jnp.arange(row_count, dtype=jnp.int32)
    frame_ok = frame_index >= 0
    row_ok = (row_index >= 0) & (row_index < row_total)
    return (frame_ok[:, None] & row_ok[None, :])[:, :, None, None]


def per_device(
    transformer_output_units,
    packed_unit_lookup,
    channel_latent_mean,
    channel_latent_deviation,
    entry_conv_weight,
    entry_conv_bias,
    group_norm_gain,
    group_norm_offset,
    residual_conv_weight,
    residual_conv_bias,
    enlarge_conv_weight,
    enlarge_conv_bias,
):
    tile_total = lax.axis_size("tile")
    unit_count = packed_unit_lookup.shape[1]
    unit_width = transformer_output_units.shape[2]
    slot_cap = 5 * unit_count // (2 * tile_total)
    targets = packed_unit_lookup[0]
    target_tile = targets // unit_count
    target_slot = targets % unit_count
    tile_match = target_tile[:, None] == jnp.arange(tile_total, dtype=jnp.int32)[None, :]
    earlier_same = jnp.cumsum(tile_match.astype(jnp.int32), axis=0) - 1
    send_rank = jnp.sum(jnp.where(tile_match, earlier_same, 0), axis=1)
    send_index = target_tile * slot_cap + send_rank
    select_dispatch = (
        jnp.arange(tile_total * slot_cap, dtype=jnp.int32)[:, None] == send_index[None, :]
    )
    send_units = jnp.dot(
        select_dispatch.astype(jnp.bfloat16),
        transformer_output_units[0],
        preferred_element_type=jnp.float32,
    ).astype(jnp.bfloat16)
    send_slots = jnp.sum(jnp.where(select_dispatch, target_slot[None, :] + 1, 0), axis=1)
    slot_lane = jnp.pad(
        send_slots.reshape(tile_total, slot_cap).astype(jnp.bfloat16),
        ((0, 0), (0, unit_width - slot_cap)),
    )
    packet = jnp.concatenate(
        [send_units.reshape(tile_total, slot_cap * unit_width), slot_lane], axis=1
    )
    got = lax.all_to_all(packet, "tile", split_axis=0, concat_axis=0, tiled=True)
    got_units = got[:, : slot_cap * unit_width].reshape(tile_total * slot_cap, unit_width)
    got_slots = got[:, slot_cap * unit_width : slot_cap * unit_width + slot_cap].astype(jnp.int32)
    choose_place = jnp.arange(1, unit_count + 1, dtype=jnp.int32)[:, None] == got_slots.reshape(
        1, -1
    )
    positioned_units = jnp.dot(
        choose_place.astype(jnp.bfloat16),
        got_units,
        preferred_element_type=jnp.float32,
    ).astype(jnp.bfloat16)
    unit_grid = positioned_units.reshape(FR_DEV, TH // 2, W // 4, 2, 2, 2, ZC)
    raw_latent = unit_grid.transpose(0, 1, 4, 2, 3, 5, 6).reshape(FR_DEV, TH, W, ZC)
    latent = (
        raw_latent.astype(jnp.float32) * channel_latent_deviation + channel_latent_mean
    ).astype(jnp.bfloat16)
    row_total = TH * tile_total
    frame_start = lax.axis_index("tm") * FR_DEV
    row_start = lax.axis_index("tile") * TH
    wide_latent = earlier_blocks(neighbour_rows(latent, 3), 2)
    hidden = causal_conv(wide_latent, entry_conv_weight, entry_conv_bias).astype(jnp.bfloat16)
    group_mean, group_scale = frame_statistics(hidden[2:, 2 : 2 + TH], row_total)
    activated = jnp.where(
        inside_mask(FR_DEV + 2, TH + 4, frame_start - 2, row_start - 2, row_total),
        normalize(hidden, group_mean, group_scale, group_norm_gain, group_norm_offset),
        0.0,
    ).astype(jnp.bfloat16)
    residual = jnp.where(
        inside_mask(FR_DEV, TH + 2, frame_start, row_start - 1, row_total),
        hidden[2:, 1 : 3 + TH].astype(jnp.float32)
        + native_causal_conv(activated, residual_conv_weight, residual_conv_bias),
        0.0,
    ).astype(jnp.bfloat16)
    return upsample_conv(residual, enlarge_conv_weight, enlarge_conv_bias)


def solution(mesh):
    placed = (
        P("tm", "tile", None),
        P("tm", "tile"),
        P(),
        P(),
        P(),
        P(),
        P(),
        P(),
        P(),
        P(),
        P(),
        P(),
    )
    return jax.shard_map(
        per_device,
        mesh=mesh,
        in_specs=placed,
        out_specs=P("tm", "tile", None, None),
        check_vma=False,
    )
```

```python
import jax
import jax.numpy as jnp
from jax import lax
from jax.sharding import PartitionSpec as P

C = 384
ZC = 16
G = 32
W = 160
FR_DEV = 2
TH = 4


def spatial_columns(framed, row_count, col_count, row_moves, col_moves):
    widened = jnp.pad(framed, ((0, 0), (0, 0), (1, 1), (0, 0)))
    return jnp.concatenate(
        [
            widened[
                :, 1 + row_move : 1 + row_move + row_count, 1 + col_move : 1 + col_move + col_count
            ]
            for row_move in row_moves
            for col_move in col_moves
        ],
        axis=3,
    )


def causal_conv(framed, weight, add_bias):
    frame_count = framed.shape[0] - 2
    row_count = framed.shape[1] - 2
    col_count = framed.shape[2]
    columns = spatial_columns(framed, row_count, col_count, (-1, 0, 1), (-1, 0, 1))
    flat_weight = weight.reshape(3, -1, weight.shape[-1])
    running = None
    for time_tap in range(3):
        tap_term = jnp.dot(
            columns[time_tap : time_tap + frame_count],
            flat_weight[time_tap],
            preferred_element_type=jnp.float32,
        )
        running = tap_term if running is None else running + tap_term
    return running + add_bias


def native_causal_conv(framed, weight, add_bias):
    result = lax.conv_general_dilated(
        framed[None],
        weight,
        window_strides=(1, 1, 1),
        padding=((0, 0), (0, 0), (1, 1)),
        dimension_numbers=("NDHWC", "DHWIO", "NDHWC"),
        preferred_element_type=jnp.float32,
    )
    return result[0] + add_bias


def phase_weights(enlarge_conv_weight):
    wide = enlarge_conv_weight.astype(jnp.float32)
    tap_groups = (((0,), (1, 2)), ((0, 1), (2,)))
    rows_a = []
    for row_phase in range(2):
        rows_b = []
        for col_phase in range(2):
            rows_u = []
            for row_off in range(2):
                rows_v = []
                for col_off in range(2):
                    total = jnp.zeros(wide.shape[2:], jnp.float32)
                    for row_tap in tap_groups[row_phase][row_off]:
                        for col_tap in tap_groups[col_phase][col_off]:
                            total = total + wide[row_tap, col_tap]
                    rows_v.append(total)
                rows_u.append(jnp.stack(rows_v))
            rows_b.append(jnp.stack(rows_u))
        rows_a.append(jnp.stack(rows_b))
    return jnp.stack(rows_a).astype(jnp.bfloat16)


def upsample_conv(framed, enlarge_conv_weight, enlarge_conv_bias):
    frame_count = framed.shape[0]
    row_count = framed.shape[1] - 2
    col_count = framed.shape[2]
    channels = framed.shape[3]
    out_channels = enlarge_conv_weight.shape[2]
    phase_weight = phase_weights(enlarge_conv_weight)
    row_phases = []
    for row_phase in range(2):
        halves = []
        for col_phase in range(2):
            row_moves = [row_phase - 1 + row_off for row_off in range(2)]
            col_moves = [col_phase - 1 + col_off for col_off in range(2)]
            columns = spatial_columns(framed, row_count, col_count, row_moves, col_moves)
            flat_weight = (
                phase_weight[row_phase, col_phase]
                .transpose(0, 1, 3, 2)
                .reshape(4 * channels, out_channels)
            )
            halves.append(
                jnp.dot(columns, flat_weight, preferred_element_type=jnp.float32)
                + enlarge_conv_bias
            )
        row_phases.append(jnp.concatenate(halves, axis=3).astype(jnp.bfloat16))
    return jnp.stack(row_phases, axis=2).reshape(
        frame_count, 2 * row_count, col_count, 2 * out_channels
    )


def neighbour_rows(latent, reach):
    tile_count = lax.axis_size("tile")
    rows = latent.shape[1]
    from_above = lax.ppermute(
        lax.slice_in_dim(latent, rows - reach, rows, axis=1),
        "tile",
        [(j, j + 1) for j in range(tile_count - 1)],
    )
    from_below = lax.ppermute(
        lax.slice_in_dim(latent, 0, reach, axis=1),
        "tile",
        [(j + 1, j) for j in range(tile_count - 1)],
    )
    return jnp.concatenate([from_above, latent, from_below], axis=1)


def earlier_blocks(features, depth):
    tm_count = lax.axis_size("tm")
    parts = [
        lax.ppermute(features, "tm", [(k, k + back) for k in range(tm_count - back)])
        for back in range(depth, 0, -1)
    ]
    return jnp.concatenate(parts + [features], axis=0)


def frame_statistics(own_hidden, row_total):
    frame_count = own_hidden.shape[0]
    block_total = lax.axis_size("tm")
    tile_count = lax.axis_size("tile")
    block_index = lax.axis_index("tm")
    grouped = own_hidden.astype(jnp.float32).reshape(frame_count, -1, G, C // G)
    local = jnp.stack(
        [jnp.sum(grouped, axis=(1, 3)), jnp.sum(grouped * grouped, axis=(1, 3))]
    ).reshape(1, -1)
    spread = jnp.broadcast_to(local, (block_total * tile_count, local.shape[1]))
    gathered = lax.all_to_all(spread, ("tm", "tile"), 0, 0, tiled=True)
    block_sums = jnp.sum(gathered.reshape(block_total, tile_count, 2, frame_count, G), axis=1)
    frame_sums = block_sums.transpose(1, 0, 2, 3).reshape(2, block_total * frame_count, G)
    running = jnp.concatenate(
        [jnp.zeros((2, 2, G), jnp.float32), jnp.cumsum(frame_sums, axis=1)], axis=1
    )
    window = lax.dynamic_slice_in_dim(running, block_index * frame_count, frame_count + 2, axis=1)
    frame_index = block_index * frame_count - 2 + jnp.arange(frame_count + 2, dtype=jnp.int32)
    cell_count = (
        jnp.maximum(frame_index + 1, 1) * (row_total * own_hidden.shape[2] * (C // G))
    ).astype(jnp.float32)[:, None]
    group_mean = window[0] / cell_count
    group_var = window[1] / cell_count - group_mean * group_mean
    return (group_mean, lax.rsqrt(jnp.maximum(group_var, 0.0) + 1e-05))


def normalize(features, group_mean, group_scale, group_norm_gain, group_norm_offset):
    repeat_count = features.shape[3] // group_mean.shape[1]
    mean_wide = jnp.repeat(group_mean, repeat_count, axis=1)[:, None, None, :]
    scale_wide = jnp.repeat(group_scale, repeat_count, axis=1)[:, None, None, :]
    scaled = (
        features.astype(jnp.float32) - mean_wide
    ) * scale_wide * group_norm_gain + group_norm_offset
    return jax.nn.silu(scaled)


def inside_mask(frame_count, row_count, frame_start, row_start, row_total):
    frame_index = frame_start + jnp.arange(frame_count, dtype=jnp.int32)
    row_index = row_start + jnp.arange(row_count, dtype=jnp.int32)
    frame_ok = frame_index >= 0
    row_ok = (row_index >= 0) & (row_index < row_total)
    return (frame_ok[:, None] & row_ok[None, :])[:, :, None, None]


def per_device(
    transformer_output_units,
    packed_unit_lookup,
    channel_latent_mean,
    channel_latent_deviation,
    entry_conv_weight,
    entry_conv_bias,
    group_norm_gain,
    group_norm_offset,
    residual_conv_weight,
    residual_conv_bias,
    enlarge_conv_weight,
    enlarge_conv_bias,
):
    tile_total = lax.axis_size("tile")
    unit_count = packed_unit_lookup.shape[1]
    unit_width = transformer_output_units.shape[2]
    slot_cap = 5 * unit_count // (2 * tile_total)
    reach = 3 * slot_cap
    targets = packed_unit_lookup[0]
    target_tile = targets // unit_count
    target_slot = targets % unit_count
    tile_match = target_tile[:, None] == jnp.arange(tile_total, dtype=jnp.int32)[None, :]
    earlier_same = jnp.cumsum(tile_match.astype(jnp.int32), axis=0) - 1
    send_rank = jnp.sum(jnp.where(tile_match, earlier_same, 0), axis=1)
    shift = jnp.arange(-1, 2, dtype=jnp.int32)[:, None]
    dest = target_tile[None, :] + shift
    send_index = jnp.where(
        (dest >= 0) & (dest < tile_total),
        dest * reach + (1 - shift) * slot_cap + send_rank[None, :],
        -1,
    )
    select_dispatch = (
        jnp.arange(tile_total * reach, dtype=jnp.int32)[:, None, None] == send_index[None, :, :]
    )
    send_units = jnp.dot(
        jnp.sum(select_dispatch.astype(jnp.bfloat16), axis=1),
        transformer_output_units[0],
        preferred_element_type=jnp.float32,
    ).astype(jnp.bfloat16)
    send_slots = jnp.sum(jnp.where(select_dispatch, target_slot[None, None, :] + 1, 0), axis=(1, 2))
    send_parts = jnp.sum(jnp.where(select_dispatch, 1 - shift[None], 0), axis=(1, 2))
    slot_lane = jnp.pad(
        jnp.concatenate(
            [send_slots.reshape(tile_total, reach), send_parts.reshape(tile_total, reach)], axis=1
        ).astype(jnp.bfloat16),
        ((0, 0), (0, unit_width - 2 * reach)),
    )
    packet = jnp.concatenate(
        [send_units.reshape(tile_total, reach * unit_width), slot_lane], axis=1
    )
    got = lax.all_to_all(packet, "tile", split_axis=0, concat_axis=0, tiled=True)
    got_units = got[:, : reach * unit_width].reshape(tile_total * reach, unit_width)
    info = got[:, reach * unit_width :].astype(jnp.int32)
    got_place = info[:, reach : 2 * reach] * unit_count + info[:, :reach]
    choose_place = jnp.arange(1, 3 * unit_count + 1, dtype=jnp.int32)[
        :, None
    ] == got_place.reshape(1, -1)
    positioned_units = jnp.dot(
        choose_place.astype(jnp.bfloat16),
        got_units,
        preferred_element_type=jnp.float32,
    ).astype(jnp.bfloat16)
    unit_grid = positioned_units.reshape(3, FR_DEV, TH // 2, W // 4, 2, 2, 2, ZC)
    raw_latent = unit_grid.transpose(1, 0, 2, 5, 3, 4, 6, 7).reshape(FR_DEV, 3 * TH, W, ZC)
    raw_latent = raw_latent[:, 1 : 3 * TH - 1]
    row_total = TH * tile_total
    frame_start = lax.axis_index("tm") * FR_DEV
    row_start = lax.axis_index("tile") * TH
    latent = jnp.where(
        inside_mask(FR_DEV, TH + 6, frame_start, row_start - 3, row_total),
        raw_latent.astype(jnp.float32) * channel_latent_deviation + channel_latent_mean,
        0.0,
    ).astype(jnp.bfloat16)
    wide_latent = earlier_blocks(latent, 2)
    hidden = causal_conv(wide_latent, entry_conv_weight, entry_conv_bias).astype(jnp.bfloat16)
    group_mean, group_scale = frame_statistics(hidden[2:, 2 : 2 + TH], row_total)
    activated = jnp.where(
        inside_mask(FR_DEV + 2, TH + 4, frame_start - 2, row_start - 2, row_total),
        normalize(hidden, group_mean, group_scale, group_norm_gain, group_norm_offset),
        0.0,
    ).astype(jnp.bfloat16)
    residual = jnp.where(
        inside_mask(FR_DEV, TH + 2, frame_start, row_start - 1, row_total),
        hidden[2:, 1 : 3 + TH].astype(jnp.float32)
        + native_causal_conv(activated, residual_conv_weight, residual_conv_bias),
        0.0,
    ).astype(jnp.bfloat16)
    return upsample_conv(residual, enlarge_conv_weight, enlarge_conv_bias)


def solution(mesh):
    placed = (
        P("tm", "tile", None),
        P("tm", "tile"),
        P(),
        P(),
        P(),
        P(),
        P(),
        P(),
        P(),
        P(),
        P(),
        P(),
    )
    return jax.shard_map(
        per_device,
        mesh=mesh,
        in_specs=placed,
        out_specs=P("tm", "tile", None, None),
        check_vma=False,
    )
```

```python
import jax
import jax.numpy as jnp
from jax import lax
from jax.sharding import PartitionSpec as P

C = 384
ZC = 16
G = 32
W = 160
FR_DEV = 2
TH = 4


def spatial_columns(framed, row_count, col_count, row_moves, col_moves):
    widened = jnp.pad(framed, ((0, 0), (0, 0), (1, 1), (0, 0)))
    return jnp.concatenate(
        [
            widened[
                :, 1 + row_move : 1 + row_move + row_count, 1 + col_move : 1 + col_move + col_count
            ]
            for row_move in row_moves
            for col_move in col_moves
        ],
        axis=3,
    )


def causal_conv(framed, weight, add_bias):
    frame_count = framed.shape[0] - 2
    row_count = framed.shape[1] - 2
    col_count = framed.shape[2]
    columns = spatial_columns(framed, row_count, col_count, (-1, 0, 1), (-1, 0, 1))
    flat_weight = weight.reshape(3, -1, weight.shape[-1])
    running = None
    for time_tap in range(3):
        tap_term = jnp.dot(
            columns[time_tap : time_tap + frame_count],
            flat_weight[time_tap],
            preferred_element_type=jnp.float32,
        )
        running = tap_term if running is None else running + tap_term
    return running + add_bias


def native_causal_conv(framed, weight, add_bias):
    result = lax.conv_general_dilated(
        framed[None],
        weight,
        window_strides=(1, 1, 1),
        padding=((0, 0), (0, 0), (1, 1)),
        dimension_numbers=("NDHWC", "DHWIO", "NDHWC"),
        preferred_element_type=jnp.float32,
    )
    return result[0] + add_bias


def phase_weights(enlarge_conv_weight):
    wide = enlarge_conv_weight.astype(jnp.float32)
    tap_groups = (((0,), (1, 2)), ((0, 1), (2,)))
    rows_a = []
    for row_phase in range(2):
        rows_b = []
        for col_phase in range(2):
            rows_u = []
            for row_off in range(2):
                rows_v = []
                for col_off in range(2):
                    total = jnp.zeros(wide.shape[2:], jnp.float32)
                    for row_tap in tap_groups[row_phase][row_off]:
                        for col_tap in tap_groups[col_phase][col_off]:
                            total = total + wide[row_tap, col_tap]
                    rows_v.append(total)
                rows_u.append(jnp.stack(rows_v))
            rows_b.append(jnp.stack(rows_u))
        rows_a.append(jnp.stack(rows_b))
    return jnp.stack(rows_a).astype(jnp.bfloat16)


def upsample_conv(framed, enlarge_conv_weight, enlarge_conv_bias):
    frame_count = framed.shape[0]
    row_count = framed.shape[1] - 2
    col_count = framed.shape[2]
    channels = framed.shape[3]
    out_channels = enlarge_conv_weight.shape[2]
    phase_weight = phase_weights(enlarge_conv_weight)
    row_phases = []
    for row_phase in range(2):
        halves = []
        for col_phase in range(2):
            row_moves = [row_phase - 1 + row_off for row_off in range(2)]
            col_moves = [col_phase - 1 + col_off for col_off in range(2)]
            columns = spatial_columns(framed, row_count, col_count, row_moves, col_moves)
            flat_weight = (
                phase_weight[row_phase, col_phase]
                .transpose(0, 1, 3, 2)
                .reshape(4 * channels, out_channels)
            )
            halves.append(
                jnp.dot(columns, flat_weight, preferred_element_type=jnp.float32)
                + enlarge_conv_bias
            )
        row_phases.append(jnp.concatenate(halves, axis=3).astype(jnp.bfloat16))
    return jnp.stack(row_phases, axis=2).reshape(
        frame_count, 2 * row_count, col_count, 2 * out_channels
    )


def neighbour_rows(latent, reach):
    tile_count = lax.axis_size("tile")
    rows = latent.shape[1]
    from_above = lax.ppermute(
        lax.slice_in_dim(latent, rows - reach, rows, axis=1),
        "tile",
        [(j, j + 1) for j in range(tile_count - 1)],
    )
    from_below = lax.ppermute(
        lax.slice_in_dim(latent, 0, reach, axis=1),
        "tile",
        [(j + 1, j) for j in range(tile_count - 1)],
    )
    return jnp.concatenate([from_above, latent, from_below], axis=1)


def earlier_blocks(features, depth):
    tm_count = lax.axis_size("tm")
    parts = [
        lax.ppermute(features, "tm", [(k, k + back) for k in range(tm_count - back)])
        for back in range(depth, 0, -1)
    ]
    return jnp.concatenate(parts + [features], axis=0)


def frame_statistics(own_hidden, row_total):
    frame_count = own_hidden.shape[0]
    block_total = lax.axis_size("tm")
    tile_count = lax.axis_size("tile")
    block_index = lax.axis_index("tm")
    grouped = own_hidden.astype(jnp.float32).reshape(frame_count, -1, G, C // G)
    local = jnp.stack(
        [jnp.sum(grouped, axis=(1, 3)), jnp.sum(grouped * grouped, axis=(1, 3))]
    ).reshape(1, -1)
    spread = jnp.broadcast_to(local, (block_total * tile_count, local.shape[1]))
    gathered = lax.all_to_all(spread, ("tm", "tile"), 0, 0, tiled=True)
    block_sums = jnp.sum(gathered.reshape(block_total, tile_count, 2, frame_count, G), axis=1)
    frame_sums = block_sums.transpose(1, 0, 2, 3).reshape(2, block_total * frame_count, G)
    running = jnp.concatenate(
        [jnp.zeros((2, 2, G), jnp.float32), jnp.cumsum(frame_sums, axis=1)], axis=1
    )
    window = lax.dynamic_slice_in_dim(running, block_index * frame_count, frame_count + 2, axis=1)
    frame_index = block_index * frame_count - 2 + jnp.arange(frame_count + 2, dtype=jnp.int32)
    cell_count = (
        jnp.maximum(frame_index + 1, 1) * (row_total * own_hidden.shape[2] * (C // G))
    ).astype(jnp.float32)[:, None]
    group_mean = window[0] / cell_count
    group_var = window[1] / cell_count - group_mean * group_mean
    return (group_mean, lax.rsqrt(jnp.maximum(group_var, 0.0) + 1e-05))


def normalize(features, group_mean, group_scale, group_norm_gain, group_norm_offset):
    repeat_count = features.shape[3] // group_mean.shape[1]
    mean_wide = jnp.repeat(group_mean, repeat_count, axis=1)[:, None, None, :]
    scale_wide = jnp.repeat(group_scale, repeat_count, axis=1)[:, None, None, :]
    scaled = (
        features.astype(jnp.float32) - mean_wide
    ) * scale_wide * group_norm_gain + group_norm_offset
    return jax.nn.silu(scaled)


def inside_mask(frame_count, row_count, frame_start, row_start, row_total):
    frame_index = frame_start + jnp.arange(frame_count, dtype=jnp.int32)
    row_index = row_start + jnp.arange(row_count, dtype=jnp.int32)
    frame_ok = frame_index >= 0
    row_ok = (row_index >= 0) & (row_index < row_total)
    return (frame_ok[:, None] & row_ok[None, :])[:, :, None, None]


def per_device(
    transformer_output_units,
    packed_unit_lookup,
    channel_latent_mean,
    channel_latent_deviation,
    entry_conv_weight,
    entry_conv_bias,
    group_norm_gain,
    group_norm_offset,
    residual_conv_weight,
    residual_conv_bias,
    enlarge_conv_weight,
    enlarge_conv_bias,
):
    tile_total = lax.axis_size("tile")
    unit_count = packed_unit_lookup.shape[1]
    unit_width = transformer_output_units.shape[2]
    slot_cap = 5 * unit_count // (2 * tile_total)
    reach = 3 * slot_cap
    targets = packed_unit_lookup[0]
    target_tile = targets // unit_count
    target_slot = targets % unit_count
    order = jnp.arange(unit_count, dtype=jnp.int32)
    send_rank = jnp.sum(
        (target_tile[:, None] == target_tile[None, :]) & (order[None, :] < order[:, None]), axis=1
    )
    shift = jnp.arange(-1, 2, dtype=jnp.int32)[:, None]
    dest = target_tile[None, :] + shift
    send_index = jnp.where(
        (dest >= 0) & (dest < tile_total),
        dest * reach + (1 - shift) * slot_cap + send_rank[None, :],
        -1,
    )
    select_dispatch = (
        jnp.arange(tile_total * reach, dtype=jnp.int32)[:, None] == send_index.reshape(1, -1)
    )
    unit_rows = jnp.concatenate(
        [
            jnp.broadcast_to(transformer_output_units[0], (3, unit_count, unit_width)),
            jnp.broadcast_to((target_slot + 1)[None, :, None], (3, unit_count, 1)).astype(jnp.bfloat16),
            jnp.broadcast_to(1 - shift[:, :, None], (3, unit_count, 1)).astype(jnp.bfloat16),
        ],
        axis=2,
    ).reshape(3 * unit_count, unit_width + 2)
    sent = jnp.dot(
        select_dispatch.astype(jnp.bfloat16), unit_rows, preferred_element_type=jnp.float32
    ).astype(jnp.bfloat16)
    slot_lane = jnp.pad(
        sent[:, unit_width:].reshape(tile_total, reach, 2).transpose(0, 2, 1).reshape(tile_total, -1),
        ((0, 0), (0, unit_width - 2 * reach)),
    )
    packet = jnp.concatenate(
        [sent[:, :unit_width].reshape(tile_total, reach * unit_width), slot_lane], axis=1
    )
    got = lax.all_to_all(packet, "tile", split_axis=0, concat_axis=0, tiled=True)
    got_units = got[:, : reach * unit_width].reshape(tile_total * reach, unit_width)
    info = got[:, reach * unit_width :].astype(jnp.int32)
    got_place = info[:, reach : 2 * reach] * unit_count + info[:, :reach]
    choose_place = jnp.arange(1, 3 * unit_count + 1, dtype=jnp.int32)[
        :, None
    ] == got_place.reshape(1, -1)
    positioned_units = jnp.dot(
        choose_place.astype(jnp.bfloat16),
        got_units,
        preferred_element_type=jnp.float32,
    ).astype(jnp.bfloat16)
    unit_grid = positioned_units.reshape(3, FR_DEV, TH // 2, W // 4, 2, 2, 2, ZC)
    raw_latent = unit_grid.transpose(1, 0, 2, 5, 3, 4, 6, 7).reshape(FR_DEV, 3 * TH, W, ZC)
    raw_latent = raw_latent[:, 1 : 3 * TH - 1]
    row_total = TH * tile_total
    frame_start = lax.axis_index("tm") * FR_DEV
    row_start = lax.axis_index("tile") * TH
    latent = jnp.where(
        inside_mask(FR_DEV, TH + 6, frame_start, row_start - 3, row_total),
        raw_latent.astype(jnp.float32) * channel_latent_deviation + channel_latent_mean,
        0.0,
    ).astype(jnp.bfloat16)
    wide_latent = earlier_blocks(latent, 2)
    hidden = causal_conv(wide_latent, entry_conv_weight, entry_conv_bias).astype(jnp.bfloat16)
    group_mean, group_scale = frame_statistics(hidden[2:, 2 : 2 + TH], row_total)
    activated = jnp.where(
        inside_mask(FR_DEV + 2, TH + 4, frame_start - 2, row_start - 2, row_total),
        normalize(hidden, group_mean, group_scale, group_norm_gain, group_norm_offset),
        0.0,
    ).astype(jnp.bfloat16)
    residual = jnp.where(
        inside_mask(FR_DEV, TH + 2, frame_start, row_start - 1, row_total),
        hidden[2:, 1 : 3 + TH].astype(jnp.float32)
        + native_causal_conv(activated, residual_conv_weight, residual_conv_bias),
        0.0,
    ).astype(jnp.bfloat16)
    return upsample_conv(residual, enlarge_conv_weight, enlarge_conv_bias)


def solution(mesh):
    placed = (
        P("tm", "tile", None),
        P("tm", "tile"),
        P(),
        P(),
        P(),
        P(),
        P(),
        P(),
        P(),
        P(),
        P(),
        P(),
    )
    return jax.shard_map(
        per_device,
        mesh=mesh,
        in_specs=placed,
        out_specs=P("tm", "tile", None, None),
        check_vma=False,
    )
```

```python
import jax
import jax.numpy as jnp
from jax import lax
from jax.sharding import PartitionSpec as P

C = 384
ZC = 16
G = 32
W = 160
FR_DEV = 2
TH = 4


def spatial_columns(framed, row_count, col_count, row_moves, col_moves):
    widened = jnp.pad(framed, ((0, 0), (0, 0), (1, 1), (0, 0)))
    return jnp.concatenate(
        [
            widened[
                :, 1 + row_move : 1 + row_move + row_count, 1 + col_move : 1 + col_move + col_count
            ]
            for row_move in row_moves
            for col_move in col_moves
        ],
        axis=3,
    )


def causal_conv(framed, weight, add_bias):
    frame_count = framed.shape[0] - 2
    row_count = framed.shape[1] - 2
    col_count = framed.shape[2]
    columns = spatial_columns(framed, row_count, col_count, (-1, 0, 1), (-1, 0, 1))
    flat_weight = weight.reshape(3, -1, weight.shape[-1])
    running = None
    for time_tap in range(3):
        tap_term = jnp.dot(
            columns[time_tap : time_tap + frame_count],
            flat_weight[time_tap],
            preferred_element_type=jnp.float32,
        )
        running = tap_term if running is None else running + tap_term
    return running + add_bias


def native_causal_conv(framed, weight, add_bias):
    result = lax.conv_general_dilated(
        framed[None],
        weight,
        window_strides=(1, 1, 1),
        padding=((0, 0), (0, 0), (1, 1)),
        dimension_numbers=("NDHWC", "DHWIO", "NDHWC"),
        preferred_element_type=jnp.float32,
    )
    return result[0] + add_bias


def phase_weights(enlarge_conv_weight):
    wide = enlarge_conv_weight.astype(jnp.float32)
    tap_groups = (((0,), (1, 2)), ((0, 1), (2,)))
    rows_a = []
    for row_phase in range(2):
        rows_b = []
        for col_phase in range(2):
            rows_u = []
            for row_off in range(2):
                rows_v = []
                for col_off in range(2):
                    total = jnp.zeros(wide.shape[2:], jnp.float32)
                    for row_tap in tap_groups[row_phase][row_off]:
                        for col_tap in tap_groups[col_phase][col_off]:
                            total = total + wide[row_tap, col_tap]
                    rows_v.append(total)
                rows_u.append(jnp.stack(rows_v))
            rows_b.append(jnp.stack(rows_u))
        rows_a.append(jnp.stack(rows_b))
    return jnp.stack(rows_a).astype(jnp.bfloat16)


def upsample_conv(framed, enlarge_conv_weight, enlarge_conv_bias):
    frame_count = framed.shape[0]
    row_count = framed.shape[1] - 2
    col_count = framed.shape[2]
    channels = framed.shape[3]
    out_channels = enlarge_conv_weight.shape[2]
    phase_weight = phase_weights(enlarge_conv_weight)
    row_phases = []
    for row_phase in range(2):
        halves = []
        for col_phase in range(2):
            row_moves = [row_phase - 1 + row_off for row_off in range(2)]
            col_moves = [col_phase - 1 + col_off for col_off in range(2)]
            columns = spatial_columns(framed, row_count, col_count, row_moves, col_moves)
            flat_weight = (
                phase_weight[row_phase, col_phase]
                .transpose(0, 1, 3, 2)
                .reshape(4 * channels, out_channels)
            )
            halves.append(
                jnp.dot(columns, flat_weight, preferred_element_type=jnp.float32)
                + enlarge_conv_bias
            )
        row_phases.append(jnp.concatenate(halves, axis=3).astype(jnp.bfloat16))
    return jnp.stack(row_phases, axis=2).reshape(
        frame_count, 2 * row_count, col_count, 2 * out_channels
    )


def neighbour_rows(latent, reach):
    tile_count = lax.axis_size("tile")
    rows = latent.shape[1]
    from_above = lax.ppermute(
        lax.slice_in_dim(latent, rows - reach, rows, axis=1),
        "tile",
        [(j, j + 1) for j in range(tile_count - 1)],
    )
    from_below = lax.ppermute(
        lax.slice_in_dim(latent, 0, reach, axis=1),
        "tile",
        [(j + 1, j) for j in range(tile_count - 1)],
    )
    return jnp.concatenate([from_above, latent, from_below], axis=1)


def earlier_blocks(features, depth):
    tm_count = lax.axis_size("tm")
    flat = features.reshape(features.shape[0], features.shape[1], -1)
    parts = [
        lax.ppermute(flat, "tm", [(k, k + back) for k in range(tm_count - back)]).reshape(
            features.shape
        )
        for back in range(depth, 0, -1)
    ]
    return jnp.concatenate(parts + [features], axis=0)


def frame_statistics(own_hidden, row_total):
    frame_count = own_hidden.shape[0]
    block_total = lax.axis_size("tm")
    tile_count = lax.axis_size("tile")
    block_index = lax.axis_index("tm")
    grouped = own_hidden.astype(jnp.float32).reshape(frame_count, -1, G, C // G)
    local = jnp.stack(
        [jnp.sum(grouped, axis=(1, 3)), jnp.sum(grouped * grouped, axis=(1, 3))]
    ).reshape(1, -1)
    spread = jnp.broadcast_to(local, (block_total * tile_count, local.shape[1]))
    gathered = lax.all_to_all(spread, ("tm", "tile"), 0, 0, tiled=True)
    block_sums = jnp.sum(gathered.reshape(block_total, tile_count, 2, frame_count, G), axis=1)
    frame_sums = block_sums.transpose(1, 0, 2, 3).reshape(2, block_total * frame_count, G)
    running = jnp.concatenate(
        [jnp.zeros((2, 2, G), jnp.float32), jnp.cumsum(frame_sums, axis=1)], axis=1
    )
    window = lax.dynamic_slice_in_dim(running, block_index * frame_count, frame_count + 2, axis=1)
    frame_index = block_index * frame_count - 2 + jnp.arange(frame_count + 2, dtype=jnp.int32)
    cell_count = (
        jnp.maximum(frame_index + 1, 1) * (row_total * own_hidden.shape[2] * (C // G))
    ).astype(jnp.float32)[:, None]
    group_mean = window[0] / cell_count
    group_var = window[1] / cell_count - group_mean * group_mean
    return (group_mean, lax.rsqrt(jnp.maximum(group_var, 0.0) + 1e-05))


def normalize(features, group_mean, group_scale, group_norm_gain, group_norm_offset):
    repeat_count = features.shape[3] // group_mean.shape[1]
    mean_wide = jnp.repeat(group_mean, repeat_count, axis=1)[:, None, None, :]
    scale_wide = jnp.repeat(group_scale, repeat_count, axis=1)[:, None, None, :]
    scaled = (
        features.astype(jnp.float32) - mean_wide
    ) * scale_wide * group_norm_gain + group_norm_offset
    return jax.nn.silu(scaled)


def inside_mask(frame_count, row_count, frame_start, row_start, row_total):
    frame_index = frame_start + jnp.arange(frame_count, dtype=jnp.int32)
    row_index = row_start + jnp.arange(row_count, dtype=jnp.int32)
    frame_ok = frame_index >= 0
    row_ok = (row_index >= 0) & (row_index < row_total)
    return (frame_ok[:, None] & row_ok[None, :])[:, :, None, None]


def per_device(
    transformer_output_units,
    packed_unit_lookup,
    channel_latent_mean,
    channel_latent_deviation,
    entry_conv_weight,
    entry_conv_bias,
    group_norm_gain,
    group_norm_offset,
    residual_conv_weight,
    residual_conv_bias,
    enlarge_conv_weight,
    enlarge_conv_bias,
):
    tile_total = lax.axis_size("tile")
    unit_count = packed_unit_lookup.shape[1]
    unit_width = transformer_output_units.shape[2]
    slot_cap = 5 * unit_count // (2 * tile_total)
    reach = 3 * slot_cap
    targets = packed_unit_lookup[0]
    target_tile = targets // unit_count
    target_slot = targets % unit_count
    tile_match = target_tile[:, None] == jnp.arange(tile_total, dtype=jnp.int32)[None, :]
    earlier_same = jnp.cumsum(tile_match.astype(jnp.int32), axis=0) - 1
    send_rank = jnp.sum(jnp.where(tile_match, earlier_same, 0), axis=1)
    shift = jnp.arange(-1, 2, dtype=jnp.int32)[:, None]
    dest = target_tile[None, :] + shift
    send_index = jnp.where(
        (dest >= 0) & (dest < tile_total),
        dest * reach + (1 - shift) * slot_cap + send_rank[None, :],
        -1,
    )
    select_dispatch = (
        jnp.arange(tile_total * reach, dtype=jnp.int32)[:, None, None] == send_index[None, :, :]
    )
    send_units = jnp.dot(
        jnp.sum(select_dispatch.astype(jnp.bfloat16), axis=1),
        transformer_output_units[0],
        preferred_element_type=jnp.float32,
    ).astype(jnp.bfloat16)
    send_slots = jnp.sum(jnp.where(select_dispatch, target_slot[None, None, :] + 1, 0), axis=(1, 2))
    send_parts = jnp.sum(jnp.where(select_dispatch, 1 - shift[None], 0), axis=(1, 2))
    slot_lane = jnp.pad(
        jnp.concatenate(
            [send_slots.reshape(tile_total, reach), send_parts.reshape(tile_total, reach)], axis=1
        ).astype(jnp.bfloat16),
        ((0, 0), (0, unit_width - 2 * reach)),
    )
    packet = jnp.concatenate(
        [send_units.reshape(tile_total, reach * unit_width), slot_lane], axis=1
    )
    got = lax.all_to_all(packet, "tile", split_axis=0, concat_axis=0, tiled=True)
    got_units = got[:, : reach * unit_width].reshape(tile_total * reach, unit_width)
    info = got[:, reach * unit_width :].astype(jnp.int32)
    got_place = info[:, reach : 2 * reach] * unit_count + info[:, :reach]
    choose_place = jnp.arange(1, 3 * unit_count + 1, dtype=jnp.int32)[
        :, None
    ] == got_place.reshape(1, -1)
    positioned_units = jnp.dot(
        choose_place.astype(jnp.bfloat16),
        got_units,
        preferred_element_type=jnp.float32,
    ).astype(jnp.bfloat16)
    unit_grid = positioned_units.reshape(3, FR_DEV, TH // 2, W // 4, 2, 2, 2, ZC)
    raw_latent = unit_grid.transpose(1, 0, 2, 5, 3, 4, 6, 7).reshape(FR_DEV, 3 * TH, W, ZC)
    raw_latent = raw_latent[:, 1 : 3 * TH - 1]
    row_total = TH * tile_total
    frame_start = lax.axis_index("tm") * FR_DEV
    row_start = lax.axis_index("tile") * TH
    latent = jnp.where(
        inside_mask(FR_DEV, TH + 6, frame_start, row_start - 3, row_total),
        raw_latent.astype(jnp.float32) * channel_latent_deviation + channel_latent_mean,
        0.0,
    ).astype(jnp.bfloat16)
    wide_latent = earlier_blocks(latent, 2)
    hidden = causal_conv(wide_latent, entry_conv_weight, entry_conv_bias).astype(jnp.bfloat16)
    group_mean, group_scale = frame_statistics(hidden[2:, 2 : 2 + TH], row_total)
    activated = jnp.where(
        inside_mask(FR_DEV + 2, TH + 4, frame_start - 2, row_start - 2, row_total),
        normalize(hidden, group_mean, group_scale, group_norm_gain, group_norm_offset),
        0.0,
    ).astype(jnp.bfloat16)
    residual = jnp.where(
        inside_mask(FR_DEV, TH + 2, frame_start, row_start - 1, row_total),
        hidden[2:, 1 : 3 + TH].astype(jnp.float32)
        + native_causal_conv(activated, residual_conv_weight, residual_conv_bias),
        0.0,
    ).astype(jnp.bfloat16)
    return upsample_conv(residual, enlarge_conv_weight, enlarge_conv_bias)


def solution(mesh):
    placed = (
        P("tm", "tile", None),
        P("tm", "tile"),
        P(),
        P(),
        P(),
        P(),
        P(),
        P(),
        P(),
        P(),
        P(),
        P(),
    )
    return jax.shard_map(
        per_device,
        mesh=mesh,
        in_specs=placed,
        out_specs=P("tm", "tile", None, None),
        check_vma=False,
    )
```
